512 devices in a mesh: seq: 32 (over y, x), tensor: 8 (over z), dp: 2 (over core).
Axes of the slice: x: 4, y: 8, z: 8, core: 2. Of those that a mesh axis runs over, the one named last changes fastest.
Arguments:
- x_stream: bfloat16 [32768, 5120], P(('dp', 'seq'), 'tensor'), parts along dimension 0
- bc_stream: bfloat16 [32768, 256], P(('dp', 'seq')), parts along dimension 0, may hold values from -6 to 6
- z_gate: bfloat16 [32768, 5120], P(('dp', 'seq'), 'tensor'), parts along dimension 0
- dt_stream: bfloat16 [80, 32768], P('tensor', ('dp', 'seq')), parts along dimension 1, as said below
- doc_ids: int32 [32768], P(('dp', 'seq')), parts along dimension 0, may hold values from 0 to 7, never falling along the last dimension, each value on 1 to 8192 neighbouring positions
- conv_x: bfloat16 [4, 5120], P(None, 'tensor'), may hold values from -3 to 3
- conv_bc: bfloat16 [4, 256], replicated, may hold values from -3 to 3
- a_log: float32 [80], P('tensor')
- dt_bias: float32 [80], P('tensor'), as said below
- d_skip: float32 [80], P('tensor'), may hold values from 0.5 to 4
- norm_gain: float32 [5120], P('tensor'), may hold values from 0.5 to 1.5
- w_out: bfloat16 [5120, 2560], P('tensor'), may hold values from -0.078125 to 0.078125
Outputs:
- layer_out: bfloat16 [32768, 2560], P(('dp', 'seq'), 'tensor'), parts along dimension 0
The draws below stay inside these ranges and needn't reach their ends.
There are 2 independent parts, one for each index of `dp`. The reference program is written for one: setup_inputs(seed, part) draws one part's arguments, and reference() takes and returns one part's arrays. A program takes and returns all parts, laid end to end along the dimension named above; an argument that names none is the same for every part. Nothing has to cross between parts.
Inputs may be any that keep to these rules, and one draw needn't show every extreme that they name: `doc_ids`: document ids never fall along the tokens; each document has 1 to 8192 tokens and one has exactly 8192. `dt_bias`: step size bias. `dt_stream`: step size logits.
All inputs are finite; a program needn't handle non-finite values.
Results may differ from the reference program's by a relative error of at most 0.017.
Values may be sent and summed in bfloat16 or wider, within the bound.
No kernel may reach another device: no remote copies, remote signals or barrier semaphores. Data moves between devices by JAX's collectives and lax.ppermute only.
A program may use at most 64 MiB of HBM per device.

```python
import math
import jax
import jax.numpy as jnp
import numpy as np
from jax import lax

D = 2560
HEADS = 80
HEADDIM = 64
NSTATE = 128
SPAN = 256
KCONV = 4
TOK_DEV = 512
DOCS = 8
INNER = 5120
TOKENS = 16384
MOST = 8192
N_TENSOR = 8


def head_law(key):
    folded = jax.random.fold_in(key, 7)
    chooser, step_key, rapid_key, steady_key = jax.random.split(folded, 4)
    portion = 0.5
    rapid_mask = jax.random.uniform(chooser, (HEADS,), jnp.float32) < portion
    base_step = jnp.exp(jax.random.uniform(step_key, (HEADS,), jnp.float32, math.log(0.02), math.log(0.1)))
    rapid_rate = jnp.exp(jax.random.uniform(rapid_key, (HEADS,), jnp.float32, math.log(0.02), math.log(0.033)))
    steady = jnp.exp(jax.random.uniform(steady_key, (HEADS,), jnp.float32, math.log(0.2), math.log(1.0)))
    strength = jnp.where(rapid_mask, rapid_rate / base_step, steady / (base_step * TOKENS))
    return (jnp.log(strength), jnp.log(jnp.expm1(base_step)))


def draw_a_log(key, part):
    return head_law(key)[0].astype(jnp.float32)


def draw_dt_bias(key, part):
    return head_law(key)[1].astype(jnp.float32)


def draw_dt_stream(key, part):
    noise_key, block_key, drop_key, depth_key = jax.random.split(jax.random.fold_in(key, 13), 4)
    shard_count = TOKENS // TOK_DEV
    noise = 0.4 * jax.random.normal(noise_key, (HEADS, TOKENS), jnp.float32)
    shifts = jax.random.uniform(block_key, (HEADS, shard_count), jnp.float32, -0.5, 0.5)
    lowered = jax.random.uniform(drop_key, (HEADS, shard_count), jnp.float32) < 0.7
    depth = jax.random.uniform(depth_key, (HEADS, shard_count), jnp.float32, -6.0, -3.0)
    shifts = shifts + jnp.where(lowered, depth, 0.0)
    return (noise + jnp.repeat(shifts, TOK_DEV, axis=1)).astype(jnp.bfloat16)


def draw_x_stream(key, part):
    noise_key = jax.random.fold_in(key, 19)
    shard_count = TOKENS // TOK_DEV
    noise = jnp.clip(jax.random.normal(noise_key, (TOKENS, INNER), jnp.float32), -6.0, 6.0)
    position = (jnp.arange(TOKENS, dtype=jnp.int32) // TOK_DEV).astype(jnp.float32)
    level = 0.03 * jnp.exp(-math.log(3.0) * position / max(shard_count - 1, 1))
    return (noise * level[:, None]).astype(jnp.bfloat16)


def draw_z_gate(key, part):
    noise_key, row_key = jax.random.split(jax.random.fold_in(key, 17), 2)
    columns = jnp.arange(INNER, dtype=jnp.float32) / INNER
    column_scale = 10.0 ** columns
    noise = jax.random.normal(noise_key, (TOKENS, INNER), jnp.float32)
    row_scale = 10.0 ** jax.random.uniform(row_key, (TOKENS, 1), jnp.float32)
    return (noise * column_scale[None, :] * row_scale).astype(jnp.bfloat16)


def block_levels(rng, extent, cuts, least, top_value):
    gain = 1.0
    for dim, parts in cuts:
        draws = jax.random.uniform(jax.random.fold_in(jax.random.fold_in(rng, 6), dim), (parts,), jnp.float32, least / len(cuts), top_value / len(cuts))
        gain = gain * jnp.repeat(jnp.exp(draws), extent[dim] // parts).reshape((-1,) + (1,) * (len(extent) - 1 - dim))
    return gain


def split_up(count, total, bound, slope):
    loads = [(1 << 20) // math.isqrt(rank ** slope) + 1 for rank in range(2, count + 1)]
    spare, counts = total - bound - (count - 1), [1] * (count - 1)
    while spare > 0:
        free = [i for i in range(count - 1) if counts[i] < bound]
        whole, budget = sum([loads[i] for i in free]), spare
        for i in free:
            addition = min(bound - counts[i], max(1, budget * loads[i] // whole), spare)
            counts[i] = counts[i] + addition
            spare = spare - addition
    return np.array([bound] + counts)


def uneven_parts(stream_key, amount, total, most, skew):
    if amount == 2:
        one = jax.random.randint(stream_key, (), max(1, total - most), min(most, total - 1) + 1)
        return jnp.stack([one, total - one])
    tallies = jnp.asarray(split_up(amount, total, most, skew), jnp.int32)
    twos = (amount - 1) // 2
    donor, sink = tallies[1:1 + 2 * twos:2], tallies[2:2 + 2 * twos:2]
    room = jnp.minimum(donor - 1, most - sink)
    moved = jax.random.randint(jax.random.fold_in(stream_key, 1), (twos,), 0, 1 << 20) % (room + 1)
    tallies = tallies.at[1:1 + 2 * twos:2].set(donor - moved).at[2:2 + 2 * twos:2].set(sink + moved)
    return tallies[jax.random.permutation(jax.random.fold_in(stream_key, 2), amount)]


def centred(own_key, extent, width, reach, pieces=(), held_as=jnp.bfloat16):
    gain = block_levels(own_key, extent, pieces, -0.22, 0.18) if pieces else 1.0
    result = jax.random.normal(own_key, extent, jnp.float32) * width * gain
    return jnp.minimum(jnp.maximum(result, -reach), reach).astype(held_as)


def setup_inputs(seed: int = 0, part: int = 0) -> dict:
    splits = jax.random.split(jax.random.key(seed), 13)
    part_splits = jax.random.split(jax.random.fold_in(splits[12], part), 13)
    return {
        "x_stream": draw_x_stream(jax.random.fold_in(jax.random.fold_in(splits[12], part), 71), part),
        "bc_stream": centred(part_splits[1], (TOKENS, 2 * NSTATE), 1.0, 6.0, ((0, 32),)),
        "z_gate": draw_z_gate(jax.random.fold_in(jax.random.fold_in(splits[12], part), 71), part),
        "dt_stream": draw_dt_stream(jax.random.fold_in(jax.random.fold_in(splits[12], part), 71), part),
        "doc_ids": jnp.searchsorted(jnp.cumsum(uneven_parts(part_splits[4], DOCS, TOKENS, MOST, 2)), jnp.arange(TOKENS), side="right").astype(jnp.int32),
        "conv_x": centred(splits[5], (KCONV, INNER), KCONV ** -0.5, 3.0, ((1, 8),)),
        "conv_bc": centred(splits[6], (KCONV, 2 * NSTATE), KCONV ** -0.5, 3.0),
        "a_log": draw_a_log(jax.random.fold_in(splits[12], 71), part),
        "dt_bias": draw_dt_bias(jax.random.fold_in(splits[12], 71), part),
        "d_skip": jnp.clip(jnp.exp(math.log(4.0) - 2.0794415 * jax.random.uniform(splits[9], (HEADS,), jnp.float32) ** block_levels(splits[9], (HEADS,), ((0, 8),), -0.2, 0.2)), 0.5, 4.0),
        "norm_gain": jnp.clip(0.5 + 1.0 * jax.random.uniform(splits[10], (INNER,), jnp.float32) ** block_levels(splits[10], (INNER,), ((0, 8),), -0.2, 0.2), 0.5, 1.5),
        "w_out": centred(splits[11], (INNER, D), INNER ** -0.5, 0.078125, ((0, 8),)),
    }


def causal_conv(values, weights, doc_ids):
    row_count = values.shape[0]
    total = jnp.zeros(values.shape, jnp.float32)
    for offset in range(KCONV):
        shifted = jnp.pad(values, ((offset, 0), (0, 0)))[:row_count]
        earlier = jnp.pad(doc_ids, (offset, 0), constant_values=-1)[:row_count]
        keep_mask = earlier == doc_ids
        total = total + jnp.where(keep_mask[:, None], shifted.astype(jnp.float32) * weights[offset].astype(jnp.float32), 0.0)
    return jax.nn.silu(total).astype(jnp.bfloat16)

def reference(x_stream, bc_stream, z_gate, dt_stream, doc_ids, conv_x, conv_bc, a_log, dt_bias, d_skip, norm_gain, w_out):
    highest = lax.Precision.HIGHEST
    mixed_x = lax.optimization_barrier(causal_conv(x_stream, conv_x, doc_ids))
    mixed_bc = lax.optimization_barrier(causal_conv(bc_stream, conv_bc, doc_ids))
    step_size = jax.nn.softplus(dt_stream.astype(jnp.float32) + dt_bias[:, None])
    log_rates = -jnp.exp(a_log)[:, None] * step_size
    blocks = TOKENS // SPAN
    block_x = mixed_x.reshape(blocks, SPAN, HEADS, HEADDIM)
    b_vals = mixed_bc[:, :NSTATE].reshape(blocks, SPAN, NSTATE)
    c_vals = mixed_bc[:, NSTATE:].reshape(blocks, SPAN, NSTATE)
    block_steps = step_size.reshape(HEADS, blocks, SPAN).transpose(1, 0, 2)
    block_rates = log_rates.reshape(HEADS, blocks, SPAN).transpose(1, 0, 2)
    block_ids = doc_ids.reshape(blocks, SPAN)
    before = jnp.concatenate([jnp.full((1,), -1, jnp.int32), doc_ids[SPAN - 1::SPAN][:blocks - 1].astype(jnp.int32)])
    lower_mask = jnp.tril(jnp.ones((SPAN, SPAN), jnp.bool_))

    def advance(carry_state, inputs_now):
        x_blk, b_blk, c_blk, dt_blk, rate_blk, id_blk, prior = inputs_now
        cum_rates = jnp.cumsum(rate_blk, axis=1)
        same_doc = (id_blk[:, None] == id_blk[None, :]) & lower_mask
        spread = cum_rates[:, :, None] - cum_rates[:, None, :]
        decay_now = jnp.where(same_doc[None], jnp.exp(jnp.minimum(spread, 0.0)), 0.0)
        b_wide = b_blk.astype(jnp.float32)
        c_wide = c_blk.astype(jnp.float32)
        x_wide = x_blk.astype(jnp.float32)
        scores = jnp.dot(c_wide, b_wide.T, precision=highest)
        weights = lax.optimization_barrier((scores[None] * decay_now * dt_blk[:, None, :]).astype(jnp.bfloat16)).astype(jnp.float32)
        diagonal = jnp.einsum('hts,shp->thp', weights, x_wide, precision=highest)
        carried = id_blk == prior
        entry_gain = jnp.where(carried[None], jnp.exp(cum_rates), 0.0)
        reach_term = jnp.einsum('tn,hpn->thp', c_wide, carry_state, precision=highest) * entry_gain.T[:, :, None]
        tail_weight = jnp.where((id_blk == id_blk[-1])[None], jnp.exp(cum_rates[:, -1:] - cum_rates), 0.0) * dt_blk
        fresh_state = jnp.einsum('shp,sn->hpn', x_wide * tail_weight.T[:, :, None], b_wide, precision=highest)
        block_decay = jnp.where(carried[-1], jnp.exp(cum_rates[:, -1]), 0.0)
        y_block = diagonal + reach_term + d_skip[None, :, None] * x_wide
        next_state = block_decay[:, None, None] * carry_state + fresh_state
        return (next_state, y_block.astype(jnp.bfloat16).reshape(SPAN, INNER))
    start_state = jnp.zeros((HEADS, HEADDIM, NSTATE), jnp.float32)
    final_state, y_all = lax.scan(advance, start_state, (block_x, b_vals, c_vals, block_steps, block_rates, block_ids, before))
    y_vals = lax.optimization_barrier(y_all.reshape(TOKENS, INNER))
    gated = y_vals.astype(jnp.float32) * jax.nn.silu(z_gate.astype(jnp.float32))
    inv_norm = lax.rsqrt(lax.optimization_barrier(jnp.mean(gated * gated, axis=1)) + 1e-05)
    normed = (gated * inv_norm[:, None] * norm_gain[None, :]).astype(jnp.bfloat16)
    group_width = INNER // N_TENSOR
    total = jnp.zeros((TOKENS, D), jnp.float32)
    for member in range(N_TENSOR):
        lower = member * group_width
        product = jnp.dot(normed[:, lower:lower + group_width], w_out[lower:lower + group_width], preferred_element_type=jnp.float32)
        total = total + lax.optimization_barrier(product.astype(jnp.bfloat16)).astype(jnp.float32)
    return total.astype(jnp.bfloat16)
```

```python
import jax
import jax.numpy as jnp
from jax import lax
from jax.sharding import PartitionSpec as P

SPAN = 256


def from_behind(block, axis, distance):
    devices = range(lax.axis_size(axis))
    route = [(i - distance, i) for i in devices if i - distance in devices]
    return lax.ppermute(block, axis, route)


def causal_conv(extended, weights, ext_ids, own_ids, row_count):
    tap_count = weights.shape[0]
    total = jnp.zeros((row_count, extended.shape[1]), jnp.float32)
    for offset in range(tap_count):
        first_row = tap_count - 1 - offset
        window = extended[first_row : first_row + row_count]
        keep_mask = ext_ids[first_row : first_row + row_count] == own_ids
        total = total + jnp.where(
            keep_mask[:, None],
            window.astype(jnp.float32) * weights[offset].astype(jnp.float32),
            0.0,
        )
    return jax.nn.silu(total).astype(jnp.bfloat16)


def pass_state(device_decay, local_final):
    shard_count = lax.axis_size("seq")
    decay, state = device_decay, local_final
    window = 1
    while 2 * window < shard_count - 1:
        prev_decay, prev_state = from_behind((decay, state.astype(jnp.bfloat16)), "seq", window)
        state = decay[:, None, None] * prev_state.astype(jnp.float32) + state
        decay = decay * prev_decay
        window *= 2
    near_decay, near_state = from_behind((decay, state.astype(jnp.bfloat16)), "seq", 1)
    if window + 1 < shard_count:
        far_state = from_behind(state.astype(jnp.bfloat16), "seq", window + 1)
        return near_decay[:, None, None] * far_state.astype(jnp.float32) + near_state.astype(
            jnp.float32
        )
    return near_state.astype(jnp.float32)


def local(
    x_stream,
    bc_stream,
    z_gate,
    dt_stream,
    doc_ids,
    conv_x,
    conv_bc,
    a_log,
    dt_bias,
    d_skip,
    norm_gain,
    w_out,
):
    highest = lax.Precision.HIGHEST
    row_count = x_stream.shape[0]
    head_count = dt_stream.shape[0]
    inner_width = x_stream.shape[1]
    head_size = inner_width // head_count
    state_size = bc_stream.shape[1] // 2
    tap_count = conv_x.shape[0]
    blocks = row_count // SPAN
    edge_start = row_count - tap_count + 1
    own_ids = doc_ids.astype(jnp.float32)
    rim_x, rim_bc, rim_ids = from_behind(
        (x_stream[edge_start:], bc_stream[edge_start:], own_ids[edge_start:].astype(jnp.bfloat16)),
        "seq",
        1,
    )
    ext_ids = jnp.concatenate([rim_ids.astype(jnp.float32), own_ids])
    mixed_x = causal_conv(jnp.concatenate([rim_x, x_stream]), conv_x, ext_ids, own_ids, row_count)
    mixed_bc = causal_conv(
        jnp.concatenate([rim_bc, bc_stream]), conv_bc, ext_ids, own_ids, row_count
    )
    prior_id = ext_ids[tap_count - 2]
    step_size = jax.nn.softplus(dt_stream.astype(jnp.float32) + dt_bias[:, None])
    log_rates = -jnp.exp(a_log)[:, None] * step_size
    block_steps = step_size.reshape(head_count, blocks, SPAN)
    cum_rates = jnp.cumsum(log_rates.reshape(head_count, blocks, SPAN), axis=2)
    block_x = mixed_x.reshape(blocks, SPAN, head_count, head_size)
    b_vals = mixed_bc[:, :state_size].reshape(blocks, SPAN, state_size)
    c_vals = mixed_bc[:, state_size:].reshape(blocks, SPAN, state_size)
    c_wide = c_vals.astype(jnp.float32)
    block_ids = own_ids.reshape(blocks, SPAN)
    before = jnp.concatenate([prior_id[None], own_ids[SPAN - 1 :: SPAN][: blocks - 1]])
    carried = block_ids == before[:, None]
    entry_gain = jnp.where(carried[None], jnp.exp(cum_rates), 0.0)
    tail_weight = (
        jnp.where(
            (block_ids == block_ids[:, -1:])[None], jnp.exp(cum_rates[:, :, -1:] - cum_rates), 0.0
        )
        * block_steps
    )
    weighted = block_x.astype(jnp.float32) * jnp.transpose(tail_weight, (1, 2, 0))[..., None]
    block_states = jnp.einsum(
        "cshp,csn->chpn", weighted, b_vals.astype(jnp.float32), precision=highest
    )
    block_decay = jnp.where(carried[:, -1][None], jnp.exp(cum_rates[:, :, -1]), 0.0)
    device_decay = jnp.prod(block_decay, axis=1)
    skip_term = d_skip[None, None, :, None] * block_x.astype(jnp.float32)
    zero_state = jnp.zeros((head_count, head_size, state_size), jnp.float32)

    def advance(carry_state, inputs_now):
        decay_now, fresh_state = inputs_now
        return (decay_now[:, None, None] * carry_state + fresh_state, carry_state)

    local_final, local_entries = lax.scan(advance, zero_state, (block_decay.T, block_states))
    reached = jnp.einsum("ctn,chpn->cthp", c_wide, local_entries, precision=highest)
    lower_mask = jnp.tril(jnp.ones((SPAN, SPAN), jnp.bool_))
    same_doc = (block_ids[:, :, None] == block_ids[:, None, :]) & lower_mask[None]
    spread = cum_rates[:, :, :, None] - cum_rates[:, :, None, :]
    decay_now = jnp.where(same_doc[None], jnp.exp(jnp.minimum(spread, 0.0)), 0.0)
    scores = jnp.einsum("ctn,csn->cts", c_vals, b_vals, preferred_element_type=jnp.float32)
    weights = (scores[None] * decay_now * block_steps[:, :, None, :]).astype(jnp.bfloat16)
    result = (
        jnp.einsum("hcts,cshp->cthp", weights, block_x, preferred_element_type=jnp.float32)
        + reached * jnp.transpose(entry_gain, (1, 2, 0))[..., None]
        + skip_term
    )
    incoming = pass_state(device_decay, local_final)
    prefix = jnp.cumprod(
        jnp.concatenate([jnp.ones((head_count, 1), jnp.float32), block_decay[:, :-1]], axis=1),
        axis=1,
    )
    reach_term = jnp.einsum("ctn,hpn->cthp", c_wide, incoming, precision=highest)
    result = (
        result + reach_term * jnp.transpose(entry_gain * prefix[:, :, None], (1, 2, 0))[..., None]
    )
    y_vals = lax.optimization_barrier(result.reshape(row_count, inner_width).astype(jnp.bfloat16))
    gated = y_vals.astype(jnp.float32) * jax.nn.silu(z_gate.astype(jnp.float32))
    squares = lax.psum(jnp.sum(gated * gated, axis=1), "tensor")
    inv_norm = lax.rsqrt(squares / (inner_width * lax.axis_size("tensor")) + 1e-05)
    normed = (gated * inv_norm[:, None] * norm_gain[None, :]).astype(jnp.bfloat16)
    partial_value = jnp.dot(normed, w_out, preferred_element_type=jnp.float32)
    return lax.psum_scatter(
        partial_value.astype(jnp.bfloat16), "tensor", scatter_dimension=1, tiled=True
    )


def solution(mesh):
    return jax.shard_map(
        local,
        mesh=mesh,
        in_specs=(
            P(("dp", "seq"), "tensor"),
            P(("dp", "seq"), None),
            P(("dp", "seq"), "tensor"),
            P("tensor", ("dp", "seq")),
            P(("dp", "seq")),
            P(None, "tensor"),
            P(),
            P("tensor"),
            P("tensor"),
            P("tensor"),
            P("tensor"),
            P("tensor", None),
        ),
        out_specs=P(("dp", "seq"), "tensor"),
        check_vma=False,
    )
```

```python
import jax
import jax.numpy as jnp
from jax import lax
from jax.sharding import PartitionSpec as P

SPAN = 256


def from_behind(block, axis, distance):
    devices = range(lax.axis_size(axis))
    route = [(i - distance, i) for i in devices if i - distance in devices]
    return lax.ppermute(block, axis, route)


def causal_conv(extended, weights, ext_ids, own_ids, row_count):
    tap_count = weights.shape[0]
    total = jnp.zeros((row_count, extended.shape[1]), jnp.float32)
    for offset in range(tap_count):
        first_row = tap_count - 1 - offset
        window = extended[first_row : first_row + row_count]
        keep_mask = ext_ids[first_row : first_row + row_count] == own_ids
        total = total + jnp.where(
            keep_mask[:, None],
            window.astype(jnp.float32) * weights[offset].astype(jnp.float32),
            0.0,
        )
    return jax.nn.silu(total).astype(jnp.bfloat16)


def pass_state(device_decay, local_final):
    shard_count = lax.axis_size("seq")
    decay, state = device_decay, local_final
    window = 1
    while 2 * window < shard_count - 1:
        prev_decay, prev_state = from_behind((decay, state.astype(jnp.bfloat16)), "seq", window)
        state = decay[:, None, None] * prev_state.astype(jnp.float32) + state
        decay = decay * prev_decay
        window *= 2
    near_decay, near_state = from_behind((decay, state.astype(jnp.bfloat16)), "seq", 1)
    if window + 1 < shard_count:
        far_state = from_behind(state.astype(jnp.bfloat16), "seq", window + 1)
        return near_decay[:, None, None] * far_state.astype(jnp.float32) + near_state.astype(
            jnp.float32
        )
    return near_state.astype(jnp.float32)


def local(
    x_stream,
    bc_stream,
    z_gate,
    dt_stream,
    doc_ids,
    conv_x,
    conv_bc,
    a_log,
    dt_bias,
    d_skip,
    norm_gain,
    w_out,
):
    highest = lax.Precision.HIGHEST
    row_count = x_stream.shape[0]
    head_count = dt_stream.shape[0]
    inner_width = x_stream.shape[1]
    head_size = inner_width // head_count
    state_size = bc_stream.shape[1] // 2
    tap_count = conv_x.shape[0]
    blocks = row_count // SPAN
    edge_start = row_count - tap_count + 1
    own_ids = doc_ids.astype(jnp.float32)
    rim_x, rim_bc, rim_ids = from_behind(
        (x_stream[edge_start:], bc_stream[edge_start:], own_ids[edge_start:].astype(jnp.bfloat16)),
        "seq",
        1,
    )
    ext_ids = jnp.concatenate([rim_ids.astype(jnp.float32), own_ids])
    mixed_x = causal_conv(jnp.concatenate([rim_x, x_stream]), conv_x, ext_ids, own_ids, row_count)
    mixed_bc = causal_conv(
        jnp.concatenate([rim_bc, bc_stream]), conv_bc, ext_ids, own_ids, row_count
    )
    prior_id = ext_ids[tap_count - 2]
    step_size = jax.nn.softplus(dt_stream.astype(jnp.float32) + dt_bias[:, None])
    log_rates = -jnp.exp(a_log)[:, None] * step_size
    block_steps = step_size.reshape(head_count, blocks, SPAN)
    cum_rates = jnp.cumsum(log_rates.reshape(head_count, blocks, SPAN), axis=2)
    block_x = mixed_x.reshape(blocks, SPAN, head_count, head_size)
    b_vals = mixed_bc[:, :state_size].reshape(blocks, SPAN, state_size)
    c_vals = mixed_bc[:, state_size:].reshape(blocks, SPAN, state_size)
    c_wide = c_vals.astype(jnp.float32)
    block_ids = own_ids.reshape(blocks, SPAN)
    before = jnp.concatenate([prior_id[None], own_ids[SPAN - 1 :: SPAN][: blocks - 1]])
    carried = block_ids == before[:, None]
    entry_gain = jnp.where(carried[None], jnp.exp(cum_rates), 0.0)
    tail_weight = (
        jnp.where(
            (block_ids == block_ids[:, -1:])[None], jnp.exp(cum_rates[:, :, -1:] - cum_rates), 0.0
        )
        * block_steps
    )
    weighted = block_x.astype(jnp.float32) * jnp.transpose(tail_weight, (1, 2, 0))[..., None]
    block_states = jnp.einsum(
        "cshp,csn->chpn", weighted, b_vals.astype(jnp.float32), precision=highest
    )
    block_decay = jnp.where(carried[:, -1][None], jnp.exp(cum_rates[:, :, -1]), 0.0)
    device_decay = jnp.prod(block_decay, axis=1)
    skip_term = d_skip[None, None, :, None] * block_x.astype(jnp.float32)
    zero_state = jnp.zeros((head_count, head_size, state_size), jnp.float32)
    entry_list = [zero_state]
    for block in range(blocks):
        entry_list.append(block_decay[:, block, None, None] * entry_list[-1] + block_states[block])
    local_final = entry_list[-1]
    local_entries = jnp.stack(entry_list[:-1])
    reached = jnp.einsum("ctn,chpn->cthp", c_wide, local_entries, precision=highest)
    lower_mask = jnp.tril(jnp.ones((SPAN, SPAN), jnp.bool_))
    same_doc = (block_ids[:, :, None] == block_ids[:, None, :]) & lower_mask[None]
    spread = cum_rates[:, :, :, None] - cum_rates[:, :, None, :]
    decay_now = jnp.where(same_doc[None], jnp.exp(jnp.minimum(spread, 0.0)), 0.0)
    scores = jnp.einsum("ctn,csn->cts", c_vals, b_vals, preferred_element_type=jnp.float32)
    weights = (scores[None] * decay_now * block_steps[:, :, None, :]).astype(jnp.bfloat16)
    result = (
        jnp.einsum("hcts,cshp->cthp", weights, block_x, preferred_element_type=jnp.float32)
        + reached * jnp.transpose(entry_gain, (1, 2, 0))[..., None]
        + skip_term
    )
    incoming = pass_state(device_decay, local_final)
    prefix = jnp.cumprod(
        jnp.concatenate([jnp.ones((head_count, 1), jnp.float32), block_decay[:, :-1]], axis=1),
        axis=1,
    )
    reach_term = jnp.einsum("ctn,hpn->cthp", c_wide, incoming, precision=highest)
    result = (
        result + reach_term * jnp.transpose(entry_gain * prefix[:, :, None], (1, 2, 0))[..., None]
    )
    y_vals = lax.optimization_barrier(result.reshape(row_count, inner_width).astype(jnp.bfloat16))
    gated = y_vals.astype(jnp.float32) * jax.nn.silu(z_gate.astype(jnp.float32))
    group_count = lax.axis_size("tensor")
    squares = jnp.sum(gated * gated, axis=1)
    scaled = (gated * norm_gain[None, :]).astype(jnp.bfloat16)
    out_width = w_out.shape[1] // group_count
    partial_value = jnp.einsum(
        "tc,cgk->gtk",
        scaled,
        w_out.reshape(inner_width, group_count, out_width),
        preferred_element_type=jnp.float32,
    ).astype(jnp.bfloat16)
    pad_rows = -(-row_count // out_width)
    square_rows = jnp.pad(squares, (0, pad_rows * out_width - row_count)).reshape(
        pad_rows, out_width
    )
    square_rows = jnp.broadcast_to(
        square_rows.astype(jnp.bfloat16)[None], (group_count, pad_rows, out_width)
    )
    payload = jnp.concatenate([partial_value, square_rows], axis=1)
    summed = lax.psum_scatter(payload, "tensor", scatter_dimension=0, tiled=True)[0]
    total_squares = summed[row_count:].reshape(-1)[:row_count].astype(jnp.float32)
    inv_norm = lax.rsqrt(total_squares / (inner_width * group_count) + 1e-05)
    return (summed[:row_count].astype(jnp.float32) * inv_norm[:, None]).astype(jnp.bfloat16)


def solution(mesh):
    return jax.shard_map(
        local,
        mesh=mesh,
        in_specs=(
            P(("dp", "seq"), "tensor"),
            P(("dp", "seq"), None),
            P(("dp", "seq"), "tensor"),
            P("tensor", ("dp", "seq")),
            P(("dp", "seq")),
            P(None, "tensor"),
            P(),
            P("tensor"),
            P("tensor"),
            P("tensor"),
            P("tensor"),
            P("tensor", None),
        ),
        out_specs=P(("dp", "seq"), "tensor"),
        check_vma=False,
    )
```

```python
import jax
import jax.numpy as jnp
from jax import lax
from jax.sharding import PartitionSpec as P

SPAN = 256


def from_behind(block, axis, distance):
    devices = range(lax.axis_size(axis))
    route = [(i - distance, i) for i in devices if i - distance in devices]
    return lax.ppermute(block, axis, route)


def causal_conv(extended, weights, ext_ids, own_ids, row_count):
    tap_count = weights.shape[0]
    total = jnp.zeros((row_count, extended.shape[1]), jnp.float32)
    for offset in range(tap_count):
        first_row = tap_count - 1 - offset
        window = extended[first_row : first_row + row_count]
        keep_mask = ext_ids[first_row : first_row + row_count] == own_ids
        total = total + jnp.where(
            keep_mask[:, None],
            window.astype(jnp.float32) * weights[offset].astype(jnp.float32),
            0.0,
        )
    return jax.nn.silu(total).astype(jnp.bfloat16)


def with_decay(decay, state):
    high = decay.astype(jnp.bfloat16)
    low = (decay - high.astype(jnp.float32)).astype(jnp.bfloat16)
    tail = jnp.broadcast_to(jnp.stack([high, low], 1)[:, :, None], (decay.shape[0], 2, state.shape[2]))
    return jnp.concatenate([state.astype(jnp.bfloat16), tail], axis=1)


def split_decay(packed):
    decay = packed[:, -2, 0].astype(jnp.float32) + packed[:, -1, 0].astype(jnp.float32)
    return decay, packed[:, :-2].astype(jnp.float32)


def pass_state(device_decay, local_final):
    shard_count = lax.axis_size("seq")
    decay, state = device_decay, local_final
    window = 1
    while 2 * window < shard_count - 1:
        prev_decay, prev_state = split_decay(
            from_behind(with_decay(decay, state), "seq", window)
        )
        state = decay[:, None, None] * prev_state + state
        decay = decay * prev_decay
        window *= 2
    near_decay, near_state = split_decay(from_behind(with_decay(decay, state), "seq", 1))
    if window + 1 < shard_count:
        far_state = from_behind(state.astype(jnp.bfloat16), "seq", window + 1)
        return near_decay[:, None, None] * far_state.astype(jnp.float32) + near_state
    return near_state


def local(
    x_stream,
    bc_stream,
    z_gate,
    dt_stream,
    doc_ids,
    conv_x,
    conv_bc,
    a_log,
    dt_bias,
    d_skip,
    norm_gain,
    w_out,
):
    highest = lax.Precision.HIGHEST
    row_count = x_stream.shape[0]
    head_count = dt_stream.shape[0]
    inner_width = x_stream.shape[1]
    head_size = inner_width // head_count
    state_size = bc_stream.shape[1] // 2
    tap_count = conv_x.shape[0]
    blocks = row_count // SPAN
    edge_start = row_count - tap_count + 1
    own_ids = doc_ids.astype(jnp.float32)
    x_width = x_stream.shape[1]
    bc_width = bc_stream.shape[1]
    rim = from_behind(
        jnp.concatenate(
            [
                x_stream[edge_start:],
                bc_stream[edge_start:],
                jnp.broadcast_to(own_ids[edge_start:, None], (tap_count - 1, 128)).astype(
                    jnp.bfloat16
                ),
            ],
            axis=1,
        ),
        "seq",
        1,
    )
    rim_x = rim[:, :x_width]
    rim_bc = rim[:, x_width : x_width + bc_width]
    rim_ids = rim[:, x_width + bc_width]
    ext_ids = jnp.concatenate([rim_ids.astype(jnp.float32), own_ids])
    mixed_x = causal_conv(jnp.concatenate([rim_x, x_stream]), conv_x, ext_ids, own_ids, row_count)
    mixed_bc = causal_conv(
        jnp.concatenate([rim_bc, bc_stream]), conv_bc, ext_ids, own_ids, row_count
    )
    prior_id = ext_ids[tap_count - 2]
    step_size = jax.nn.softplus(dt_stream.astype(jnp.float32) + dt_bias[:, None])
    log_rates = -jnp.exp(a_log)[:, None] * step_size
    block_steps = step_size.reshape(head_count, blocks, SPAN)
    cum_rates = jnp.cumsum(log_rates.reshape(head_count, blocks, SPAN), axis=2)
    block_x = mixed_x.reshape(blocks, SPAN, head_count, head_size)
    b_vals = mixed_bc[:, :state_size].reshape(blocks, SPAN, state_size)
    c_vals = mixed_bc[:, state_size:].reshape(blocks, SPAN, state_size)
    c_wide = c_vals.astype(jnp.float32)
    block_ids = own_ids.reshape(blocks, SPAN)
    before = jnp.concatenate([prior_id[None], own_ids[SPAN - 1 :: SPAN][: blocks - 1]])
    carried = block_ids == before[:, None]
    entry_gain = jnp.where(carried[None], jnp.exp(cum_rates), 0.0)
    tail_weight = (
        jnp.where(
            (block_ids == block_ids[:, -1:])[None], jnp.exp(cum_rates[:, :, -1:] - cum_rates), 0.0
        )
        * block_steps
    )
    weighted = block_x.astype(jnp.float32) * jnp.transpose(tail_weight, (1, 2, 0))[..., None]
    block_states = jnp.einsum(
        "cshp,csn->chpn", weighted, b_vals.astype(jnp.float32), precision=highest
    )
    block_decay = jnp.where(carried[:, -1][None], jnp.exp(cum_rates[:, :, -1]), 0.0)
    device_decay = jnp.prod(block_decay, axis=1)
    skip_term = d_skip[None, None, :, None] * block_x.astype(jnp.float32)
    zero_state = jnp.zeros((head_count, head_size, state_size), jnp.float32)
    entry_list = [zero_state]
    for block in range(blocks):
        entry_list.append(block_decay[:, block, None, None] * entry_list[-1] + block_states[block])
    local_final = entry_list[-1]
    local_entries = jnp.stack(entry_list[:-1])
    reached = jnp.einsum("ctn,chpn->cthp", c_wide, local_entries, precision=highest)
    lower_mask = jnp.tril(jnp.ones((SPAN, SPAN), jnp.bool_))
    same_doc = (block_ids[:, :, None] == block_ids[:, None, :]) & lower_mask[None]
    spread = cum_rates[:, :, :, None] - cum_rates[:, :, None, :]
    decay_now = jnp.where(same_doc[None], jnp.exp(jnp.minimum(spread, 0.0)), 0.0)
    scores = jnp.einsum("ctn,csn->cts", c_vals, b_vals, preferred_element_type=jnp.float32)
    weights = (scores[None] * decay_now * block_steps[:, :, None, :]).astype(jnp.bfloat16)
    result = (
        jnp.einsum("hcts,cshp->cthp", weights, block_x, preferred_element_type=jnp.float32)
        + reached * jnp.transpose(entry_gain, (1, 2, 0))[..., None]
        + skip_term
    )
    incoming = pass_state(device_decay, local_final)
    prefix = jnp.cumprod(
        jnp.concatenate([jnp.ones((head_count, 1), jnp.float32), block_decay[:, :-1]], axis=1),
        axis=1,
    )
    reach_term = jnp.einsum("ctn,hpn->cthp", c_wide, incoming, precision=highest)
    result = (
        result + reach_term * jnp.transpose(entry_gain * prefix[:, :, None], (1, 2, 0))[..., None]
    )
    y_vals = lax.optimization_barrier(result.reshape(row_count, inner_width).astype(jnp.bfloat16))
    gated = y_vals.astype(jnp.float32) * jax.nn.silu(z_gate.astype(jnp.float32))
    group_count = lax.axis_size("tensor")
    squares = jnp.sum(gated * gated, axis=1)
    scaled = (gated * norm_gain[None, :]).astype(jnp.bfloat16)
    out_width = w_out.shape[1] // group_count
    partial_value = jnp.einsum(
        "tc,cgk->gtk",
        scaled,
        w_out.reshape(inner_width, group_count, out_width),
        preferred_element_type=jnp.float32,
    ).astype(jnp.bfloat16)
    pad_rows = -(-row_count // out_width)
    square_rows = jnp.pad(squares, (0, pad_rows * out_width - row_count)).reshape(
        pad_rows, out_width
    )
    square_rows = jnp.broadcast_to(
        square_rows.astype(jnp.bfloat16)[None], (group_count, pad_rows, out_width)
    )
    payload = jnp.concatenate([partial_value, square_rows], axis=1)
    summed = lax.psum_scatter(payload, "tensor", scatter_dimension=0, tiled=True)[0]
    total_squares = summed[row_count:].reshape(-1)[:row_count].astype(jnp.float32)
    inv_norm = lax.rsqrt(total_squares / (inner_width * group_count) + 1e-05)
    return (summed[:row_count].astype(jnp.float32) * inv_norm[:, None]).astype(jnp.bfloat16)


def solution(mesh):
    return jax.shard_map(
        local,
        mesh=mesh,
        in_specs=(
            P(("dp", "seq"), "tensor"),
            P(("dp", "seq"), None),
            P(("dp", "seq"), "tensor"),
            P("tensor", ("dp", "seq")),
            P(("dp", "seq")),
            P(None, "tensor"),
            P(),
            P("tensor"),
            P("tensor"),
            P("tensor"),
            P("tensor"),
            P("tensor", None),
        ),
        out_specs=P(("dp", "seq"), "tensor"),
        check_vma=False,
    )
```

```python
import jax
import jax.numpy as jnp
from jax import lax
from jax.sharding import PartitionSpec as P

SPAN = 256


def from_behind(block, axis, distance):
    devices = range(lax.axis_size(axis))
    route = [(i - distance, i) for i in devices if i - distance in devices]
    return lax.ppermute(block, axis, route)


def causal_conv(extended, weights, ext_ids, own_ids, row_count):
    tap_count = weights.shape[0]
    total = jnp.zeros((row_count, extended.shape[1]), jnp.float32)
    for offset in range(tap_count):
        first_row = tap_count - 1 - offset
        window = extended[first_row : first_row + row_count]
        keep_mask = ext_ids[first_row : first_row + row_count] == own_ids
        total = total + jnp.where(
            keep_mask[:, None],
            window.astype(jnp.float32) * weights[offset].astype(jnp.float32),
            0.0,
        )
    return jax.nn.silu(total).astype(jnp.bfloat16)


def with_decay(decay, state):
    high = decay.astype(jnp.bfloat16)
    low = (decay - high.astype(jnp.float32)).astype(jnp.bfloat16)
    tail = jnp.broadcast_to(jnp.stack([high, low], 1)[:, :, None], (decay.shape[0], 2, state.shape[2]))
    return jnp.concatenate([state.astype(jnp.bfloat16), tail], axis=1)


def split_decay(packed):
    decay = packed[:, -2, 0].astype(jnp.float32) + packed[:, -1, 0].astype(jnp.float32)
    return decay, packed[:, :-2].astype(jnp.float32)


def pass_state(device_decay, local_final):
    shard_count = lax.axis_size("seq")
    decay, state = device_decay, local_final
    window = 1
    while 2 * window < shard_count - 1:
        prev_decay, prev_state = split_decay(
            from_behind(with_decay(decay, state), "seq", window)
        )
        state = decay[:, None, None] * prev_state + state
        decay = decay * prev_decay
        window *= 2
    near_decay, near_state = split_decay(from_behind(with_decay(decay, state), "seq", 1))
    if window + 1 < shard_count:
        far_state = from_behind(state.astype(jnp.bfloat16), "seq", window + 1)
        return near_decay[:, None, None] * far_state.astype(jnp.float32) + near_state
    return near_state


def local(
    x_stream,
    bc_stream,
    z_gate,
    dt_stream,
    doc_ids,
    conv_x,
    conv_bc,
    a_log,
    dt_bias,
    d_skip,
    norm_gain,
    w_out,
):
    highest = lax.Precision.HIGH
    row_count = x_stream.shape[0]
    head_count = dt_stream.shape[0]
    inner_width = x_stream.shape[1]
    head_size = inner_width // head_count
    state_size = bc_stream.shape[1] // 2
    tap_count = conv_x.shape[0]
    blocks = row_count // SPAN
    edge_start = row_count - tap_count + 1
    own_ids = doc_ids.astype(jnp.float32)
    x_width = x_stream.shape[1]
    bc_width = bc_stream.shape[1]
    rim = from_behind(
        jnp.concatenate(
            [
                x_stream[edge_start:],
                bc_stream[edge_start:],
                jnp.broadcast_to(own_ids[edge_start:, None], (tap_count - 1, 128)).astype(
                    jnp.bfloat16
                ),
            ],
            axis=1,
        ),
        "seq",
        1,
    )
    rim_x = rim[:, :x_width]
    rim_bc = rim[:, x_width : x_width + bc_width]
    rim_ids = rim[:, x_width + bc_width]
    ext_ids = jnp.concatenate([rim_ids.astype(jnp.float32), own_ids])
    mixed_x = causal_conv(jnp.concatenate([rim_x, x_stream]), conv_x, ext_ids, own_ids, row_count)
    mixed_bc = causal_conv(
        jnp.concatenate([rim_bc, bc_stream]), conv_bc, ext_ids, own_ids, row_count
    )
    prior_id = ext_ids[tap_count - 2]
    step_size = jax.nn.softplus(dt_stream.astype(jnp.float32) + dt_bias[:, None])
    log_rates = -jnp.exp(a_log)[:, None] * step_size
    block_steps = step_size.reshape(head_count, blocks, SPAN)
    cum_rates = jnp.cumsum(log_rates.reshape(head_count, blocks, SPAN), axis=2)
    block_x = mixed_x.reshape(blocks, SPAN, head_count, head_size)
    b_vals = mixed_bc[:, :state_size].reshape(blocks, SPAN, state_size)
    c_vals = mixed_bc[:, state_size:].reshape(blocks, SPAN, state_size)
    c_wide = c_vals.astype(jnp.float32)
    block_ids = own_ids.reshape(blocks, SPAN)
    before = jnp.concatenate([prior_id[None], own_ids[SPAN - 1 :: SPAN][: blocks - 1]])
    carried = block_ids == before[:, None]
    entry_gain = jnp.where(carried[None], jnp.exp(cum_rates), 0.0)
    tail_weight = (
        jnp.where(
            (block_ids == block_ids[:, -1:])[None], jnp.exp(cum_rates[:, :, -1:] - cum_rates), 0.0
        )
        * block_steps
    )
    weighted = block_x.astype(jnp.float32) * jnp.transpose(tail_weight, (1, 2, 0))[..., None]
    block_states = jnp.einsum(
        "cshp,csn->chpn", weighted, b_vals.astype(jnp.float32), precision=highest
    )
    block_decay = jnp.where(carried[:, -1][None], jnp.exp(cum_rates[:, :, -1]), 0.0)
    device_decay = jnp.prod(block_decay, axis=1)
    skip_term = d_skip[None, None, :, None] * block_x.astype(jnp.float32)
    zero_state = jnp.zeros((head_count, head_size, state_size), jnp.float32)
    entry_list = [zero_state]
    for block in range(blocks):
        entry_list.append(block_decay[:, block, None, None] * entry_list[-1] + block_states[block])
    local_final = entry_list[-1]
    local_entries = jnp.stack(entry_list[:-1])
    reached = jnp.einsum("ctn,chpn->cthp", c_wide, local_entries, precision=highest)
    lower_mask = jnp.tril(jnp.ones((SPAN, SPAN), jnp.bool_))
    same_doc = (block_ids[:, :, None] == block_ids[:, None, :]) & lower_mask[None]
    spread = cum_rates[:, :, :, None] - cum_rates[:, :, None, :]
    decay_now = jnp.where(same_doc[None], jnp.exp(jnp.minimum(spread, 0.0)), 0.0)
    scores = jnp.einsum("ctn,csn->cts", c_vals, b_vals, preferred_element_type=jnp.float32)
    weights = (scores[None] * decay_now * block_steps[:, :, None, :]).astype(jnp.bfloat16)
    result = (
        jnp.einsum("hcts,cshp->cthp", weights, block_x, preferred_element_type=jnp.float32)
        + reached * jnp.transpose(entry_gain, (1, 2, 0))[..., None]
        + skip_term
    )
    incoming = pass_state(device_decay, local_final)
    prefix = jnp.cumprod(
        jnp.concatenate([jnp.ones((head_count, 1), jnp.float32), block_decay[:, :-1]], axis=1),
        axis=1,
    )
    reach_term = jnp.einsum("ctn,hpn->cthp", c_wide, incoming, precision=highest)
    result = (
        result + reach_term * jnp.transpose(entry_gain * prefix[:, :, None], (1, 2, 0))[..., None]
    )
    y_vals = lax.optimization_barrier(result.reshape(row_count, inner_width).astype(jnp.bfloat16))
    gated = y_vals.astype(jnp.float32) * jax.nn.silu(z_gate.astype(jnp.float32))
    group_count = lax.axis_size("tensor")
    squares = jnp.sum(gated * gated, axis=1)
    scaled = (gated * norm_gain[None, :]).astype(jnp.bfloat16)
    out_width = w_out.shape[1] // group_count
    partial_value = jnp.dot(scaled, w_out, preferred_element_type=jnp.float32).astype(jnp.bfloat16)
    partial_value = jnp.transpose(partial_value.reshape(row_count, group_count, out_width), (1, 0, 2))
    pad_rows = -(-row_count // out_width)
    square_rows = jnp.pad(squares, (0, pad_rows * out_width - row_count)).reshape(
        pad_rows, out_width
    )
    square_rows = jnp.broadcast_to(
        square_rows.astype(jnp.bfloat16)[None], (group_count, pad_rows, out_width)
    )
    payload = jnp.concatenate([partial_value, square_rows], axis=1)
    summed = lax.psum_scatter(payload, "tensor", scatter_dimension=0, tiled=True)[0]
    total_squares = summed[row_count:].reshape(-1)[:row_count].astype(jnp.float32)
    inv_norm = lax.rsqrt(total_squares / (inner_width * group_count) + 1e-05)
    return (summed[:row_count].astype(jnp.float32) * inv_norm[:, None]).astype(jnp.bfloat16)


def solution(mesh):
    return jax.shard_map(
        local,
        mesh=mesh,
        in_specs=(
            P(("dp", "seq"), "tensor"),
            P(("dp", "seq"), None),
            P(("dp", "seq"), "tensor"),
            P("tensor", ("dp", "seq")),
            P(("dp", "seq")),
            P(None, "tensor"),
            P(),
            P("tensor"),
            P("tensor"),
            P("tensor"),
            P("tensor"),
            P("tensor", None),
        ),
        out_specs=P(("dp", "seq"), "tensor"),
        check_vma=False,
    )
```

```python
import jax
import jax.numpy as jnp
from jax import lax
from jax.sharding import PartitionSpec as P

SPAN = 256


def from_behind(block, axis, distance):
    devices = range(lax.axis_size(axis))
    route = [(i - distance, i) for i in devices if i - distance in devices]
    return lax.ppermute(block, axis, route)


def causal_conv(extended, weights, ext_ids, own_ids, row_count):
    tap_count = weights.shape[0]
    total = jnp.zeros((row_count, extended.shape[1]), jnp.float32)
    for offset in range(tap_count):
        first_row = tap_count - 1 - offset
        window = extended[first_row : first_row + row_count]
        keep_mask = ext_ids[first_row : first_row + row_count] == own_ids
        total = total + jnp.where(
            keep_mask[:, None],
            window.astype(jnp.float32) * weights[offset].astype(jnp.float32),
            0.0,
        )
    return jax.nn.silu(total).astype(jnp.bfloat16)


def with_decay(decay, state):
    high = decay.astype(jnp.bfloat16)
    low = (decay - high.astype(jnp.float32)).astype(jnp.bfloat16)
    tail = jnp.broadcast_to(jnp.stack([high, low], 1)[:, :, None], (decay.shape[0], 2, state.shape[2]))
    return jnp.concatenate([state.astype(jnp.bfloat16), tail], axis=1)


def split_decay(packed):
    decay = packed[:, -2, 0].astype(jnp.float32) + packed[:, -1, 0].astype(jnp.float32)
    return decay, packed[:, :-2].astype(jnp.float32)


def pass_state(device_decay, local_final, passengers):
    shard_count = lax.axis_size("seq")
    decay, state = device_decay, local_final
    window = 1
    while 2 * window < shard_count - 1:
        received = from_behind(with_decay(decay, state), "seq", window)
        if window == 1:
            received, passengers = lax.optimization_barrier((received, passengers))
        prev_decay, prev_state = split_decay(received)
        state = decay[:, None, None] * prev_state + state
        decay = decay * prev_decay
        window *= 2
    near_decay, near_state = split_decay(from_behind(with_decay(decay, state), "seq", 1))
    if window + 1 < shard_count:
        far_state = from_behind(state.astype(jnp.bfloat16), "seq", window + 1)
        return near_decay[:, None, None] * far_state.astype(jnp.float32) + near_state, passengers
    return near_state, passengers


def local(
    x_stream,
    bc_stream,
    z_gate,
    dt_stream,
    doc_ids,
    conv_x,
    conv_bc,
    a_log,
    dt_bias,
    d_skip,
    norm_gain,
    w_out,
):
    highest = lax.Precision.HIGHEST
    row_count = x_stream.shape[0]
    head_count = dt_stream.shape[0]
    inner_width = x_stream.shape[1]
    head_size = inner_width // head_count
    state_size = bc_stream.shape[1] // 2
    tap_count = conv_x.shape[0]
    blocks = row_count // SPAN
    edge_start = row_count - tap_count + 1
    own_ids = doc_ids.astype(jnp.float32)
    x_width = x_stream.shape[1]
    bc_width = bc_stream.shape[1]
    rim = from_behind(
        jnp.concatenate(
            [
                x_stream[edge_start:],
                bc_stream[edge_start:],
                jnp.broadcast_to(own_ids[edge_start:, None], (tap_count - 1, 128)).astype(
                    jnp.bfloat16
                ),
            ],
            axis=1,
        ),
        "seq",
        1,
    )
    rim_x = rim[:, :x_width]
    rim_bc = rim[:, x_width : x_width + bc_width]
    rim_ids = rim[:, x_width + bc_width]
    ext_ids = jnp.concatenate([rim_ids.astype(jnp.float32), own_ids])
    mixed_x = causal_conv(jnp.concatenate([rim_x, x_stream]), conv_x, ext_ids, own_ids, row_count)
    mixed_bc = causal_conv(
        jnp.concatenate([rim_bc, bc_stream]), conv_bc, ext_ids, own_ids, row_count
    )
    prior_id = ext_ids[tap_count - 2]
    step_size = jax.nn.softplus(dt_stream.astype(jnp.float32) + dt_bias[:, None])
    log_rates = -jnp.exp(a_log)[:, None] * step_size
    block_steps = step_size.reshape(head_count, blocks, SPAN)
    cum_rates = jnp.cumsum(log_rates.reshape(head_count, blocks, SPAN), axis=2)
    block_x = mixed_x.reshape(blocks, SPAN, head_count, head_size)
    b_vals = mixed_bc[:, :state_size].reshape(blocks, SPAN, state_size)
    c_vals = mixed_bc[:, state_size:].reshape(blocks, SPAN, state_size)
    c_wide = c_vals.astype(jnp.float32)
    block_ids = own_ids.reshape(blocks, SPAN)
    before = jnp.concatenate([prior_id[None], own_ids[SPAN - 1 :: SPAN][: blocks - 1]])
    carried = block_ids == before[:, None]
    entry_gain = jnp.where(carried[None], jnp.exp(cum_rates), 0.0)
    tail_weight = (
        jnp.where(
            (block_ids == block_ids[:, -1:])[None], jnp.exp(cum_rates[:, :, -1:] - cum_rates), 0.0
        )
        * block_steps
    )
    weighted = block_x.astype(jnp.float32) * jnp.transpose(tail_weight, (1, 2, 0))[..., None]
    block_states = jnp.einsum(
        "cshp,csn->chpn", weighted, b_vals.astype(jnp.float32), precision=highest
    )
    block_decay = jnp.where(carried[:, -1][None], jnp.exp(cum_rates[:, :, -1]), 0.0)
    device_decay = jnp.prod(block_decay, axis=1)
    skip_term = d_skip[None, None, :, None] * block_x.astype(jnp.float32)
    zero_state = jnp.zeros((head_count, head_size, state_size), jnp.float32)
    entry_list = [zero_state]
    for block in range(blocks):
        entry_list.append(block_decay[:, block, None, None] * entry_list[-1] + block_states[block])
    local_final = entry_list[-1]
    local_entries = jnp.stack(entry_list[:-1])
    reached = jnp.einsum("ctn,chpn->cthp", c_wide, local_entries, precision=highest)
    lower_mask = jnp.tril(jnp.ones((SPAN, SPAN), jnp.bool_))
    same_doc = (block_ids[:, :, None] == block_ids[:, None, :]) & lower_mask[None]
    spread = cum_rates[:, :, :, None] - cum_rates[:, :, None, :]
    decay_now = jnp.where(same_doc[None], jnp.exp(jnp.minimum(spread, 0.0)), 0.0)
    scores = jnp.einsum("ctn,csn->cts", c_vals, b_vals, preferred_element_type=jnp.float32)
    weights = (scores[None] * decay_now * block_steps[:, :, None, :]).astype(jnp.bfloat16)
    result = (
        jnp.einsum("hcts,cshp->cthp", weights, block_x, preferred_element_type=jnp.float32)
        + reached * jnp.transpose(entry_gain, (1, 2, 0))[..., None]
        + skip_term
    )
    incoming, (z_gate, w_out) = pass_state(device_decay, local_final, (z_gate, w_out))
    prefix = jnp.cumprod(
        jnp.concatenate([jnp.ones((head_count, 1), jnp.float32), block_decay[:, :-1]], axis=1),
        axis=1,
    )
    reach_term = jnp.einsum("ctn,hpn->cthp", c_wide, incoming, precision=highest)
    result = (
        result + reach_term * jnp.transpose(entry_gain * prefix[:, :, None], (1, 2, 0))[..., None]
    )
    y_vals = lax.optimization_barrier(result.reshape(row_count, inner_width).astype(jnp.bfloat16))
    gated = y_vals.astype(jnp.float32) * jax.nn.silu(z_gate.astype(jnp.float32))
    group_count = lax.axis_size("tensor")
    squares = jnp.sum(gated * gated, axis=1)
    scaled = (gated * norm_gain[None, :]).astype(jnp.bfloat16)
    out_width = w_out.shape[1] // group_count
    partial_value = jnp.einsum(
        "tc,cgk->gtk",
        scaled,
        w_out.reshape(inner_width, group_count, out_width),
        preferred_element_type=jnp.float32,
    ).astype(jnp.bfloat16)
    pad_rows = -(-row_count // out_width)
    square_rows = jnp.pad(squares, (0, pad_rows * out_width - row_count)).reshape(
        pad_rows, out_width
    )
    square_rows = jnp.broadcast_to(
        square_rows.astype(jnp.bfloat16)[None], (group_count, pad_rows, out_width)
    )
    payload = jnp.concatenate([partial_value, square_rows], axis=1)
    summed = lax.psum_scatter(payload, "tensor", scatter_dimension=0, tiled=True)[0]
    total_squares = summed[row_count:].reshape(-1)[:row_count].astype(jnp.float32)
    inv_norm = lax.rsqrt(total_squares / (inner_width * group_count) + 1e-05)
    return (summed[:row_count].astype(jnp.float32) * inv_norm[:, None]).astype(jnp.bfloat16)


def solution(mesh):
    return jax.shard_map(
        local,
        mesh=mesh,
        in_specs=(
            P(("dp", "seq"), "tensor"),
            P(("dp", "seq"), None),
            P(("dp", "seq"), "tensor"),
            P("tensor", ("dp", "seq")),
            P(("dp", "seq")),
            P(None, "tensor"),
            P(),
            P("tensor"),
            P("tensor"),
            P("tensor"),
            P("tensor"),
            P("tensor", None),
        ),
        out_specs=P(("dp", "seq"), "tensor"),
        check_vma=False,
    )
```

```python
import jax
import jax.numpy as jnp
from jax import lax
from jax.sharding import PartitionSpec as P

SPAN = 256


def from_behind(block, axis, distance):
    devices = range(lax.axis_size(axis))
    route = [(i - distance, i) for i in devices if i - distance in devices]
    return lax.ppermute(block, axis, route)


def causal_conv(extended, weights, ext_ids, own_ids, row_count):
    tap_count = weights.shape[0]
    total = jnp.zeros((row_count, extended.shape[1]), jnp.float32)
    for offset in range(tap_count):
        first_row = tap_count - 1 - offset
        window = extended[first_row : first_row + row_count]
        keep_mask = ext_ids[first_row : first_row + row_count] == own_ids
        total = total + jnp.where(
            keep_mask[:, None],
            window.astype(jnp.float32) * weights[offset].astype(jnp.float32),
            0.0,
        )
    return jax.nn.silu(total).astype(jnp.bfloat16)


def with_decay(decay, state):
    high = decay.astype(jnp.bfloat16)
    low = (decay - high.astype(jnp.float32)).astype(jnp.bfloat16)
    tail = jnp.broadcast_to(jnp.stack([high, low], 1)[:, :, None], (decay.shape[0], 2, state.shape[2]))
    return jnp.concatenate([state.astype(jnp.bfloat16), tail], axis=1)


def split_decay(packed):
    decay = packed[:, -2, 0].astype(jnp.float32) + packed[:, -1, 0].astype(jnp.float32)
    return decay, packed[:, :-2].astype(jnp.float32)


def pass_state(device_decay, local_final, passengers):
    shard_count = lax.axis_size("seq")
    decay, state = device_decay, local_final
    window = 1
    while 2 * window < shard_count - 1:
        received = from_behind(with_decay(decay, state), "seq", window)
        if window == 1:
            received, passengers = lax.optimization_barrier((received, passengers))
        prev_decay, prev_state = split_decay(received)
        state = decay[:, None, None] * prev_state + state
        decay = decay * prev_decay
        window *= 2
    near_decay, near_state = split_decay(from_behind(with_decay(decay, state), "seq", 1))
    if window + 1 < shard_count:
        far_state = from_behind(state.astype(jnp.bfloat16), "seq", window + 1)
        return near_decay[:, None, None] * far_state.astype(jnp.float32) + near_state, passengers
    return near_state, passengers


def local(
    x_stream,
    bc_stream,
    z_gate,
    dt_stream,
    doc_ids,
    conv_x,
    conv_bc,
    a_log,
    dt_bias,
    d_skip,
    norm_gain,
    w_out,
):
    highest = lax.Precision.HIGHEST
    row_count = x_stream.shape[0]
    head_count = dt_stream.shape[0]
    inner_width = x_stream.shape[1]
    head_size = inner_width // head_count
    state_size = bc_stream.shape[1] // 2
    tap_count = conv_x.shape[0]
    blocks = row_count // SPAN
    edge_start = row_count - tap_count + 1
    own_ids = doc_ids.astype(jnp.float32)
    x_width = x_stream.shape[1]
    bc_width = bc_stream.shape[1]
    rim = from_behind(
        jnp.concatenate(
            [
                x_stream[edge_start:],
                bc_stream[edge_start:],
                jnp.broadcast_to(own_ids[edge_start:, None], (tap_count - 1, 128)).astype(
                    jnp.bfloat16
                ),
            ],
            axis=1,
        ),
        "seq",
        1,
    )
    rim_x = rim[:, :x_width]
    rim_bc = rim[:, x_width : x_width + bc_width]
    rim_ids = rim[:, x_width + bc_width]
    ext_ids = jnp.concatenate([rim_ids.astype(jnp.float32), own_ids])
    mixed_x = causal_conv(jnp.concatenate([rim_x, x_stream]), conv_x, ext_ids, own_ids, row_count)
    mixed_bc = causal_conv(
        jnp.concatenate([rim_bc, bc_stream]), conv_bc, ext_ids, own_ids, row_count
    )
    prior_id = ext_ids[tap_count - 2]
    step_size = jax.nn.softplus(dt_stream.astype(jnp.float32) + dt_bias[:, None])
    log_rates = -jnp.exp(a_log)[:, None] * step_size
    block_steps = step_size.reshape(head_count, blocks, SPAN)
    cum_rates = jnp.cumsum(log_rates.reshape(head_count, blocks, SPAN), axis=2)
    block_x = mixed_x.reshape(blocks, SPAN, head_count, head_size)
    b_vals = mixed_bc[:, :state_size].reshape(blocks, SPAN, state_size)
    c_vals = mixed_bc[:, state_size:].reshape(blocks, SPAN, state_size)
    c_wide = c_vals.astype(jnp.float32)
    block_ids = own_ids.reshape(blocks, SPAN)
    before = jnp.concatenate([prior_id[None], own_ids[SPAN - 1 :: SPAN][: blocks - 1]])
    carried = block_ids == before[:, None]
    entry_gain = jnp.where(carried[None], jnp.exp(cum_rates), 0.0)
    tail_weight = (
        jnp.where(
            (block_ids == block_ids[:, -1:])[None], jnp.exp(cum_rates[:, :, -1:] - cum_rates), 0.0
        )
        * block_steps
    )
    weighted = block_x.astype(jnp.float32) * jnp.transpose(tail_weight, (1, 2, 0))[..., None]
    block_states = jnp.einsum(
        "cshp,csn->chpn", weighted, b_vals.astype(jnp.float32), precision=highest
    )
    block_decay = jnp.where(carried[:, -1][None], jnp.exp(cum_rates[:, :, -1]), 0.0)
    device_decay = jnp.prod(block_decay, axis=1)
    skip_term = d_skip[None, None, :, None] * block_x.astype(jnp.float32)
    zero_state = jnp.zeros((head_count, head_size, state_size), jnp.float32)
    entry_list = [zero_state]
    for block in range(blocks):
        entry_list.append(block_decay[:, block, None, None] * entry_list[-1] + block_states[block])
    local_final = entry_list[-1]
    local_entries = jnp.stack(entry_list[:-1])
    reached = jnp.einsum("ctn,chpn->cthp", c_wide, local_entries, precision=highest)
    lower_mask = jnp.tril(jnp.ones((SPAN, SPAN), jnp.bool_))
    same_doc = (block_ids[:, :, None] == block_ids[:, None, :]) & lower_mask[None]
    spread = cum_rates[:, :, :, None] - cum_rates[:, :, None, :]
    decay_now = jnp.where(same_doc[None], jnp.exp(jnp.minimum(spread, 0.0)), 0.0)
    scores = jnp.einsum("ctn,csn->cts", c_vals, b_vals, preferred_element_type=jnp.float32)
    weights = (scores[None] * decay_now * block_steps[:, :, None, :]).astype(jnp.bfloat16)
    result = (
        jnp.einsum("hcts,cshp->cthp", weights, block_x, preferred_element_type=jnp.float32)
        + reached * jnp.transpose(entry_gain, (1, 2, 0))[..., None]
        + skip_term
    )
    incoming, (z_gate, w_out) = pass_state(device_decay, local_final, (z_gate, w_out))
    prefix = jnp.cumprod(
        jnp.concatenate([jnp.ones((head_count, 1), jnp.float32), block_decay[:, :-1]], axis=1),
        axis=1,
    )
    reach_term = jnp.einsum("ctn,hpn->cthp", c_wide, incoming, precision=highest)
    result = (
        result + reach_term * jnp.transpose(entry_gain * prefix[:, :, None], (1, 2, 0))[..., None]
    )
    y_vals = lax.optimization_barrier(result.reshape(row_count, inner_width).astype(jnp.bfloat16))
    gated = y_vals.astype(jnp.float32) * jax.nn.silu(z_gate.astype(jnp.float32))
    group_count = lax.axis_size("tensor")
    squares = jnp.sum(gated * gated, axis=1)
    scaled = (gated * norm_gain[None, :]).astype(jnp.bfloat16)
    out_width = w_out.shape[1] // group_count
    partial_value = jnp.dot(scaled, w_out, preferred_element_type=jnp.float32).astype(jnp.bfloat16)
    pad_rows = -(-row_count // out_width)
    square_rows = jnp.pad(squares, (0, pad_rows * out_width - row_count)).reshape(
        pad_rows, 1, out_width
    )
    square_rows = jnp.broadcast_to(
        square_rows.astype(jnp.bfloat16), (pad_rows, group_count, out_width)
    ).reshape(pad_rows, group_count * out_width)
    payload = jnp.concatenate([partial_value, square_rows], axis=0)
    summed = lax.psum_scatter(payload, "tensor", scatter_dimension=1, tiled=True)
    total_squares = summed[row_count:].reshape(-1)[:row_count].astype(jnp.float32)
    inv_norm = lax.rsqrt(total_squares / (inner_width * group_count) + 1e-05)
    return (summed[:row_count].astype(jnp.float32) * inv_norm[:, None]).astype(jnp.bfloat16)


def solution(mesh):
    return jax.shard_map(
        local,
        mesh=mesh,
        in_specs=(
            P(("dp", "seq"), "tensor"),
            P(("dp", "seq"), None),
            P(("dp", "seq"), "tensor"),
            P("tensor", ("dp", "seq")),
            P(("dp", "seq")),
            P(None, "tensor"),
            P(),
            P("tensor"),
            P("tensor"),
            P("tensor"),
            P("tensor"),
            P("tensor", None),
        ),
        out_specs=P(("dp", "seq"), "tensor"),
        check_vma=False,
    )
```

```python
import jax
import jax.numpy as jnp
from jax import lax
from jax.sharding import PartitionSpec as P

SPAN = 256


def from_behind(block, axis, distance):
    devices = range(lax.axis_size(axis))
    route = [(i - distance, i) for i in devices if i - distance in devices]
    return lax.ppermute(block, axis, route)


def causal_conv(extended, weights, ext_ids, own_ids, row_count):
    tap_count = weights.shape[0]
    total = jnp.zeros((row_count, extended.shape[1]), jnp.float32)
    for offset in range(tap_count):
        first_row = tap_count - 1 - offset
        window = extended[first_row : first_row + row_count]
        keep_mask = ext_ids[first_row : first_row + row_count] == own_ids
        total = total + jnp.where(
            keep_mask[:, None],
            window.astype(jnp.float32) * weights[offset].astype(jnp.float32),
            0.0,
        )
    return jax.nn.silu(total).astype(jnp.bfloat16)


def with_decay(decay, state):
    high = decay.astype(jnp.bfloat16)
    low = (decay - high.astype(jnp.float32)).astype(jnp.bfloat16)
    tail = jnp.broadcast_to(jnp.stack([high, low], 1)[:, :, None], (decay.shape[0], 2, state.shape[2]))
    return jnp.concatenate([state.astype(jnp.bfloat16), tail], axis=1)


def split_decay(packed):
    decay = packed[:, -2, 0].astype(jnp.float32) + packed[:, -1, 0].astype(jnp.float32)
    return decay, packed[:, :-2].astype(jnp.float32)


def pass_state(device_decay, local_final, passengers):
    shard_count = lax.axis_size("seq")
    decay, state = device_decay, local_final
    window = 1
    while 4 * window < shard_count - 1:
        received = from_behind(with_decay(decay, state), "seq", window)
        if window == 1:
            received, passengers = lax.optimization_barrier((received, passengers))
        prev_decay, prev_state = split_decay(received)
        state = decay[:, None, None] * prev_state + state
        decay = decay * prev_decay
        window *= 2
    packed = with_decay(decay, state)
    part_count = -(-(shard_count - 1) // window)
    parts = [
        split_decay(from_behind(packed, "seq", 1 + part * window)) for part in range(part_count)
    ]
    if not parts:
        return jnp.zeros_like(local_final), passengers
    incoming_decay, incoming = parts[0]
    for part_decay, part_state in parts[1:]:
        incoming = incoming_decay[:, None, None] * part_state + incoming
        incoming_decay = incoming_decay * part_decay
    return incoming, passengers


def local(
    x_stream,
    bc_stream,
    z_gate,
    dt_stream,
    doc_ids,
    conv_x,
    conv_bc,
    a_log,
    dt_bias,
    d_skip,
    norm_gain,
    w_out,
):
    highest = lax.Precision.HIGHEST
    row_count = x_stream.shape[0]
    head_count = dt_stream.shape[0]
    inner_width = x_stream.shape[1]
    head_size = inner_width // head_count
    state_size = bc_stream.shape[1] // 2
    tap_count = conv_x.shape[0]
    blocks = row_count // SPAN
    edge_start = row_count - tap_count + 1
    own_ids = doc_ids.astype(jnp.float32)
    x_width = x_stream.shape[1]
    bc_width = bc_stream.shape[1]
    rim = from_behind(
        jnp.concatenate(
            [
                x_stream[edge_start:],
                bc_stream[edge_start:],
                jnp.broadcast_to(own_ids[edge_start:, None], (tap_count - 1, 128)).astype(
                    jnp.bfloat16
                ),
            ],
            axis=1,
        ),
        "seq",
        1,
    )
    rim_x = rim[:, :x_width]
    rim_bc = rim[:, x_width : x_width + bc_width]
    rim_ids = rim[:, x_width + bc_width]
    ext_ids = jnp.concatenate([rim_ids.astype(jnp.float32), own_ids])
    mixed_x = causal_conv(jnp.concatenate([rim_x, x_stream]), conv_x, ext_ids, own_ids, row_count)
    mixed_bc = causal_conv(
        jnp.concatenate([rim_bc, bc_stream]), conv_bc, ext_ids, own_ids, row_count
    )
    prior_id = ext_ids[tap_count - 2]
    step_size = jax.nn.softplus(dt_stream.astype(jnp.float32) + dt_bias[:, None])
    log_rates = -jnp.exp(a_log)[:, None] * step_size
    block_steps = step_size.reshape(head_count, blocks, SPAN)
    cum_rates = jnp.cumsum(log_rates.reshape(head_count, blocks, SPAN), axis=2)
    block_x = mixed_x.reshape(blocks, SPAN, head_count, head_size)
    b_vals = mixed_bc[:, :state_size].reshape(blocks, SPAN, state_size)
    c_vals = mixed_bc[:, state_size:].reshape(blocks, SPAN, state_size)
    c_wide = c_vals.astype(jnp.float32)
    block_ids = own_ids.reshape(blocks, SPAN)
    before = jnp.concatenate([prior_id[None], own_ids[SPAN - 1 :: SPAN][: blocks - 1]])
    carried = block_ids == before[:, None]
    entry_gain = jnp.where(carried[None], jnp.exp(cum_rates), 0.0)
    tail_weight = (
        jnp.where(
            (block_ids == block_ids[:, -1:])[None], jnp.exp(cum_rates[:, :, -1:] - cum_rates), 0.0
        )
        * block_steps
    )
    weighted = block_x.astype(jnp.float32) * jnp.transpose(tail_weight, (1, 2, 0))[..., None]
    block_states = jnp.einsum(
        "cshp,csn->chpn", weighted, b_vals.astype(jnp.float32), precision=highest
    )
    block_decay = jnp.where(carried[:, -1][None], jnp.exp(cum_rates[:, :, -1]), 0.0)
    device_decay = jnp.prod(block_decay, axis=1)
    skip_term = d_skip[None, None, :, None] * block_x.astype(jnp.float32)
    zero_state = jnp.zeros((head_count, head_size, state_size), jnp.float32)
    entry_list = [zero_state]
    for block in range(blocks):
        entry_list.append(block_decay[:, block, None, None] * entry_list[-1] + block_states[block])
    local_final = entry_list[-1]
    local_entries = jnp.stack(entry_list[:-1])
    reached = jnp.einsum("ctn,chpn->cthp", c_wide, local_entries, precision=highest)
    lower_mask = jnp.tril(jnp.ones((SPAN, SPAN), jnp.bool_))
    same_doc = (block_ids[:, :, None] == block_ids[:, None, :]) & lower_mask[None]
    spread = cum_rates[:, :, :, None] - cum_rates[:, :, None, :]
    decay_now = jnp.where(same_doc[None], jnp.exp(jnp.minimum(spread, 0.0)), 0.0)
    scores = jnp.einsum("ctn,csn->cts", c_vals, b_vals, preferred_element_type=jnp.float32)
    weights = (scores[None] * decay_now * block_steps[:, :, None, :]).astype(jnp.bfloat16)
    result = (
        jnp.einsum("hcts,cshp->cthp", weights, block_x, preferred_element_type=jnp.float32)
        + reached * jnp.transpose(entry_gain, (1, 2, 0))[..., None]
        + skip_term
    )
    incoming, (z_gate, w_out) = pass_state(device_decay, local_final, (z_gate, w_out))
    prefix = jnp.cumprod(
        jnp.concatenate([jnp.ones((head_count, 1), jnp.float32), block_decay[:, :-1]], axis=1),
        axis=1,
    )
    reach_term = jnp.einsum("ctn,hpn->cthp", c_wide, incoming, precision=highest)
    result = (
        result + reach_term * jnp.transpose(entry_gain * prefix[:, :, None], (1, 2, 0))[..., None]
    )
    y_vals = lax.optimization_barrier(result.reshape(row_count, inner_width).astype(jnp.bfloat16))
    gated = y_vals.astype(jnp.float32) * jax.nn.silu(z_gate.astype(jnp.float32))
    group_count = lax.axis_size("tensor")
    squares = jnp.sum(gated * gated, axis=1)
    scaled = (gated * norm_gain[None, :]).astype(jnp.bfloat16)
    out_width = w_out.shape[1] // group_count
    partial_value = jnp.einsum(
        "tc,cgk->gtk",
        scaled,
        w_out.reshape(inner_width, group_count, out_width),
        preferred_element_type=jnp.float32,
    ).astype(jnp.bfloat16)
    pad_rows = -(-row_count // out_width)
    square_rows = jnp.pad(squares, (0, pad_rows * out_width - row_count)).reshape(
        pad_rows, out_width
    )
    square_rows = jnp.broadcast_to(
        square_rows.astype(jnp.bfloat16)[None], (group_count, pad_rows, out_width)
    )
    payload = jnp.concatenate([partial_value, square_rows], axis=1)
    summed = lax.psum_scatter(payload, "tensor", scatter_dimension=0, tiled=True)[0]
    total_squares = summed[row_count:].reshape(-1)[:row_count].astype(jnp.float32)
    inv_norm = lax.rsqrt(total_squares / (inner_width * group_count) + 1e-05)
    return (summed[:row_count].astype(jnp.float32) * inv_norm[:, None]).astype(jnp.bfloat16)


def solution(mesh):
    return jax.shard_map(
        local,
        mesh=mesh,
        in_specs=(
            P(("dp", "seq"), "tensor"),
            P(("dp", "seq"), None),
            P(("dp", "seq"), "tensor"),
            P("tensor", ("dp", "seq")),
            P(("dp", "seq")),
            P(None, "tensor"),
            P(),
            P("tensor"),
            P("tensor"),
            P("tensor"),
            P("tensor"),
            P("tensor", None),
        ),
        out_specs=P(("dp", "seq"), "tensor"),
        check_vma=False,
    )
```

```python
import jax
import jax.numpy as jnp
from jax import lax
from jax.sharding import PartitionSpec as P

SPAN = 256


def from_behind(block, axis, distance):
    devices = range(lax.axis_size(axis))
    route = [(i - distance, i) for i in devices if i - distance in devices]
    return lax.ppermute(block, axis, route)


def causal_conv(extended, weights, ext_ids, own_ids, row_count):
    tap_count = weights.shape[0]
    total = jnp.zeros((row_count, extended.shape[1]), jnp.float32)
    for offset in range(tap_count):
        first_row = tap_count - 1 - offset
        window = extended[first_row : first_row + row_count]
        keep_mask = ext_ids[first_row : first_row + row_count] == own_ids
        total = total + jnp.where(
            keep_mask[:, None],
            window.astype(jnp.float32) * weights[offset].astype(jnp.float32),
            0.0,
        )
    return jax.nn.silu(total).astype(jnp.bfloat16)


def with_decay(decay, state):
    head_count = state.shape[0]
    high = decay.astype(jnp.bfloat16)
    low = (decay - high.astype(jnp.float32)).astype(jnp.bfloat16)
    tail_rows = -(-head_count // 16) * 16
    tail = jnp.pad(
        jnp.stack([high, low], 1), ((0, tail_rows - head_count), (0, state.shape[2] - 2))
    )
    flat = state.astype(jnp.bfloat16).reshape(head_count * state.shape[1], state.shape[2])
    return jnp.concatenate([flat, tail], axis=0)


def split_decay(packed, head_count, head_size):
    rows = head_count * head_size
    decay = packed[rows : rows + head_count, 0].astype(jnp.float32) + packed[
        rows : rows + head_count, 1
    ].astype(jnp.float32)
    return decay, packed[:rows].astype(jnp.float32).reshape(head_count, head_size, -1)


def pass_state(device_decay, local_final, passengers):
    shard_count = lax.axis_size("seq")
    decay, state = device_decay, local_final
    window = 1
    while 4 * window < shard_count - 1:
        received = from_behind(with_decay(decay, state), "seq", window)
        if window == 1:
            received, passengers = lax.optimization_barrier((received, passengers))
        prev_decay, prev_state = split_decay(received, *state.shape[:2])
        state = decay[:, None, None] * prev_state + state
        decay = decay * prev_decay
        window *= 2
    packed = with_decay(decay, state)
    part_count = -(-(shard_count - 1) // window)
    parts = [
        split_decay(from_behind(packed, "seq", 1 + part * window), *state.shape[:2])
        for part in range(part_count)
    ]
    if not parts:
        return jnp.zeros_like(local_final), passengers
    incoming_decay, incoming = parts[0]
    for part_decay, part_state in parts[1:]:
        incoming = incoming_decay[:, None, None] * part_state + incoming
        incoming_decay = incoming_decay * part_decay
    return incoming, passengers


def local(
    x_stream,
    bc_stream,
    z_gate,
    dt_stream,
    doc_ids,
    conv_x,
    conv_bc,
    a_log,
    dt_bias,
    d_skip,
    norm_gain,
    w_out,
):
    highest = lax.Precision.HIGHEST
    row_count = x_stream.shape[0]
    head_count = dt_stream.shape[0]
    inner_width = x_stream.shape[1]
    head_size = inner_width // head_count
    state_size = bc_stream.shape[1] // 2
    tap_count = conv_x.shape[0]
    blocks = row_count // SPAN
    edge_start = row_count - tap_count + 1
    own_ids = doc_ids.astype(jnp.float32)
    x_width = x_stream.shape[1]
    bc_width = bc_stream.shape[1]
    rim = from_behind(
        jnp.concatenate(
            [
                x_stream[edge_start:],
                bc_stream[edge_start:],
                jnp.broadcast_to(own_ids[edge_start:, None], (tap_count - 1, 128)).astype(
                    jnp.bfloat16
                ),
            ],
            axis=1,
        ),
        "seq",
        1,
    )
    rim_x = rim[:, :x_width]
    rim_bc = rim[:, x_width : x_width + bc_width]
    rim_ids = rim[:, x_width + bc_width]
    ext_ids = jnp.concatenate([rim_ids.astype(jnp.float32), own_ids])
    mixed_x = causal_conv(jnp.concatenate([rim_x, x_stream]), conv_x, ext_ids, own_ids, row_count)
    mixed_bc = causal_conv(
        jnp.concatenate([rim_bc, bc_stream]), conv_bc, ext_ids, own_ids, row_count
    )
    prior_id = ext_ids[tap_count - 2]
    step_size = jax.nn.softplus(dt_stream.astype(jnp.float32) + dt_bias[:, None])
    log_rates = -jnp.exp(a_log)[:, None] * step_size
    block_steps = step_size.reshape(head_count, blocks, SPAN)
    cum_rates = jnp.cumsum(log_rates.reshape(head_count, blocks, SPAN), axis=2)
    block_x = mixed_x.reshape(blocks, SPAN, head_count, head_size)
    b_vals = mixed_bc[:, :state_size].reshape(blocks, SPAN, state_size)
    c_vals = mixed_bc[:, state_size:].reshape(blocks, SPAN, state_size)
    c_wide = c_vals.astype(jnp.float32)
    block_ids = own_ids.reshape(blocks, SPAN)
    before = jnp.concatenate([prior_id[None], own_ids[SPAN - 1 :: SPAN][: blocks - 1]])
    carried = block_ids == before[:, None]
    entry_gain = jnp.where(carried[None], jnp.exp(cum_rates), 0.0)
    tail_weight = (
        jnp.where(
            (block_ids == block_ids[:, -1:])[None], jnp.exp(cum_rates[:, :, -1:] - cum_rates), 0.0
        )
        * block_steps
    )
    weighted = block_x.astype(jnp.float32) * jnp.transpose(tail_weight, (1, 2, 0))[..., None]
    block_states = jnp.einsum(
        "cshp,csn->chpn", weighted, b_vals.astype(jnp.float32), precision=highest
    )
    block_decay = jnp.where(carried[:, -1][None], jnp.exp(cum_rates[:, :, -1]), 0.0)
    device_decay = jnp.prod(block_decay, axis=1)
    skip_term = d_skip[None, None, :, None] * block_x.astype(jnp.float32)
    zero_state = jnp.zeros((head_count, head_size, state_size), jnp.float32)
    entry_list = [zero_state]
    for block in range(blocks):
        entry_list.append(block_decay[:, block, None, None] * entry_list[-1] + block_states[block])
    local_final = entry_list[-1]
    local_entries = jnp.stack(entry_list[:-1])
    reached = jnp.einsum("ctn,chpn->cthp", c_wide, local_entries, precision=highest)
    lower_mask = jnp.tril(jnp.ones((SPAN, SPAN), jnp.bool_))
    same_doc = (block_ids[:, :, None] == block_ids[:, None, :]) & lower_mask[None]
    spread = cum_rates[:, :, :, None] - cum_rates[:, :, None, :]
    decay_now = jnp.where(same_doc[None], jnp.exp(jnp.minimum(spread, 0.0)), 0.0)
    scores = jnp.einsum("ctn,csn->cts", c_vals, b_vals, preferred_element_type=jnp.float32)
    weights = (scores[None] * decay_now * block_steps[:, :, None, :]).astype(jnp.bfloat16)
    result = (
        jnp.einsum("hcts,cshp->cthp", weights, block_x, preferred_element_type=jnp.float32)
        + reached * jnp.transpose(entry_gain, (1, 2, 0))[..., None]
        + skip_term
    )
    incoming, (z_gate, w_out) = pass_state(device_decay, local_final, (z_gate, w_out))
    prefix = jnp.cumprod(
        jnp.concatenate([jnp.ones((head_count, 1), jnp.float32), block_decay[:, :-1]], axis=1),
        axis=1,
    )
    reach_term = jnp.einsum("ctn,hpn->cthp", c_wide, incoming, precision=highest)
    result = (
        result + reach_term * jnp.transpose(entry_gain * prefix[:, :, None], (1, 2, 0))[..., None]
    )
    y_vals = lax.optimization_barrier(result.reshape(row_count, inner_width).astype(jnp.bfloat16))
    gated = y_vals.astype(jnp.float32) * jax.nn.silu(z_gate.astype(jnp.float32))
    group_count = lax.axis_size("tensor")
    squares = jnp.sum(gated * gated, axis=1)
    scaled = (gated * norm_gain[None, :]).astype(jnp.bfloat16)
    out_width = w_out.shape[1] // group_count
    partial_value = jnp.einsum(
        "tc,cgk->gtk",
        scaled,
        w_out.reshape(inner_width, group_count, out_width),
        preferred_element_type=jnp.float32,
    ).astype(jnp.bfloat16)
    pad_rows = -(-row_count // out_width)
    square_rows = jnp.pad(squares, (0, pad_rows * out_width - row_count)).reshape(
        pad_rows, out_width
    )
    square_rows = jnp.broadcast_to(
        square_rows.astype(jnp.bfloat16)[None], (group_count, pad_rows, out_width)
    )
    payload = jnp.concatenate([partial_value, square_rows], axis=1)
    summed = lax.psum_scatter(payload, "tensor", scatter_dimension=0, tiled=True)[0]
    total_squares = summed[row_count:].reshape(-1)[:row_count].astype(jnp.float32)
    inv_norm = lax.rsqrt(total_squares / (inner_width * group_count) + 1e-05)
    return (summed[:row_count].astype(jnp.float32) * inv_norm[:, None]).astype(jnp.bfloat16)


def solution(mesh):
    return jax.shard_map(
        local,
        mesh=mesh,
        in_specs=(
            P(("dp", "seq"), "tensor"),
            P(("dp", "seq"), None),
            P(("dp", "seq"), "tensor"),
            P("tensor", ("dp", "seq")),
            P(("dp", "seq")),
            P(None, "tensor"),
            P(),
            P("tensor"),
            P("tensor"),
            P("tensor"),
            P("tensor"),
            P("tensor", None),
        ),
        out_specs=P(("dp", "seq"), "tensor"),
        check_vma=False,
    )
```

```python
import jax
import jax.numpy as jnp
from jax import lax
from jax.sharding import PartitionSpec as P

SPAN = 256


def from_behind(block, axis, distance):
    devices = range(lax.axis_size(axis))
    route = [(i - distance, i) for i in devices if i - distance in devices]
    return lax.ppermute(block, axis, route)


def causal_conv(extended, weights, ext_ids, own_ids, row_count):
    tap_count = weights.shape[0]
    total = jnp.zeros((row_count, extended.shape[1]), jnp.float32)
    for offset in range(tap_count):
        first_row = tap_count - 1 - offset
        window = extended[first_row : first_row + row_count]
        keep_mask = ext_ids[first_row : first_row + row_count] == own_ids
        total = total + jnp.where(
            keep_mask[:, None],
            window.astype(jnp.float32) * weights[offset].astype(jnp.float32),
            0.0,
        )
    return jax.nn.silu(total).astype(jnp.bfloat16)


def with_decay(decay, state):
    head_count = state.shape[0]
    high = decay.astype(jnp.bfloat16)
    low = (decay - high.astype(jnp.float32)).astype(jnp.bfloat16)
    tail_rows = -(-head_count // 16) * 16
    tail = jnp.pad(
        jnp.stack([high, low], 1), ((0, tail_rows - head_count), (0, state.shape[2] - 2))
    )
    flat = state.astype(jnp.bfloat16).reshape(head_count * state.shape[1], state.shape[2])
    return jnp.concatenate([flat, tail], axis=0)


def split_decay(packed, head_count, head_size):
    rows = head_count * head_size
    decay = packed[rows : rows + head_count, 0].astype(jnp.float32) + packed[
        rows : rows + head_count, 1
    ].astype(jnp.float32)
    return decay, packed[:rows].astype(jnp.float32).reshape(head_count, head_size, -1)


def pass_state(device_decay, local_final, passengers, prepare):
    shard_count = lax.axis_size("seq")
    decay, state = device_decay, local_final
    window = 1
    while 4 * window < shard_count - 1:
        sent = with_decay(decay, state)
        if window == 1:
            sent, passengers = lax.optimization_barrier((sent, passengers))
        received = from_behind(sent, "seq", window)
        if window == 1:
            received, passengers = lax.optimization_barrier((received, prepare(passengers)))
        prev_decay, prev_state = split_decay(received, *state.shape[:2])
        state = decay[:, None, None] * prev_state + state
        decay = decay * prev_decay
        window *= 2
    packed = with_decay(decay, state)
    part_count = -(-(shard_count - 1) // window)
    parts = [
        split_decay(from_behind(packed, "seq", 1 + part * window), *state.shape[:2])
        for part in range(part_count)
    ]
    if not parts:
        return jnp.zeros_like(local_final), passengers
    incoming_decay, incoming = parts[0]
    for part_decay, part_state in parts[1:]:
        incoming = incoming_decay[:, None, None] * part_state + incoming
        incoming_decay = incoming_decay * part_decay
    return incoming, passengers


def local(
    x_stream,
    bc_stream,
    z_gate,
    dt_stream,
    doc_ids,
    conv_x,
    conv_bc,
    a_log,
    dt_bias,
    d_skip,
    norm_gain,
    w_out,
):
    highest = lax.Precision.HIGHEST
    row_count = x_stream.shape[0]
    head_count = dt_stream.shape[0]
    inner_width = x_stream.shape[1]
    head_size = inner_width // head_count
    state_size = bc_stream.shape[1] // 2
    tap_count = conv_x.shape[0]
    blocks = row_count // SPAN
    edge_start = row_count - tap_count + 1
    own_ids = doc_ids.astype(jnp.float32)
    x_width = x_stream.shape[1]
    bc_width = bc_stream.shape[1]
    rim = from_behind(
        jnp.concatenate(
            [
                x_stream[edge_start:],
                bc_stream[edge_start:],
                jnp.broadcast_to(own_ids[edge_start:, None], (tap_count - 1, 128)).astype(
                    jnp.bfloat16
                ),
            ],
            axis=1,
        ),
        "seq",
        1,
    )
    rim_x = rim[:, :x_width]
    rim_bc = rim[:, x_width : x_width + bc_width]
    rim_ids = rim[:, x_width + bc_width]
    ext_ids = jnp.concatenate([rim_ids.astype(jnp.float32), own_ids])
    mixed_x = causal_conv(jnp.concatenate([rim_x, x_stream]), conv_x, ext_ids, own_ids, row_count)
    mixed_bc = causal_conv(
        jnp.concatenate([rim_bc, bc_stream]), conv_bc, ext_ids, own_ids, row_count
    )
    prior_id = ext_ids[tap_count - 2]
    step_size = jax.nn.softplus(dt_stream.astype(jnp.float32) + dt_bias[:, None])
    log_rates = -jnp.exp(a_log)[:, None] * step_size
    block_steps = step_size.reshape(head_count, blocks, SPAN)
    cum_rates = jnp.cumsum(log_rates.reshape(head_count, blocks, SPAN), axis=2)
    block_x = mixed_x.reshape(blocks, SPAN, head_count, head_size)
    b_vals = mixed_bc[:, :state_size].reshape(blocks, SPAN, state_size)
    c_vals = mixed_bc[:, state_size:].reshape(blocks, SPAN, state_size)
    c_wide = c_vals.astype(jnp.float32)
    block_ids = own_ids.reshape(blocks, SPAN)
    before = jnp.concatenate([prior_id[None], own_ids[SPAN - 1 :: SPAN][: blocks - 1]])
    carried = block_ids == before[:, None]
    entry_gain = jnp.where(carried[None], jnp.exp(cum_rates), 0.0)
    tail_weight = (
        jnp.where(
            (block_ids == block_ids[:, -1:])[None], jnp.exp(cum_rates[:, :, -1:] - cum_rates), 0.0
        )
        * block_steps
    )
    weighted = block_x.astype(jnp.float32) * jnp.transpose(tail_weight, (1, 2, 0))[..., None]
    block_states = jnp.einsum(
        "cshp,csn->chpn", weighted, b_vals.astype(jnp.float32), precision=highest
    )
    block_decay = jnp.where(carried[:, -1][None], jnp.exp(cum_rates[:, :, -1]), 0.0)
    device_decay = jnp.prod(block_decay, axis=1)
    skip_term = d_skip[None, None, :, None] * block_x.astype(jnp.float32)
    zero_state = jnp.zeros((head_count, head_size, state_size), jnp.float32)
    entry_list = [zero_state]
    for block in range(blocks):
        entry_list.append(block_decay[:, block, None, None] * entry_list[-1] + block_states[block])
    local_final = entry_list[-1]
    local_entries = jnp.stack(entry_list[:-1])
    reached = jnp.einsum("ctn,chpn->cthp", c_wide, local_entries, precision=highest)
    lower_mask = jnp.tril(jnp.ones((SPAN, SPAN), jnp.bool_))
    same_doc = (block_ids[:, :, None] == block_ids[:, None, :]) & lower_mask[None]
    spread = cum_rates[:, :, :, None] - cum_rates[:, :, None, :]
    decay_now = jnp.where(same_doc[None], jnp.exp(jnp.minimum(spread, 0.0)), 0.0)
    scores = jnp.einsum("ctn,csn->cts", c_vals, b_vals, preferred_element_type=jnp.float32)
    weights = (scores[None] * decay_now * block_steps[:, :, None, :]).astype(jnp.bfloat16)
    result = (
        jnp.einsum("hcts,cshp->cthp", weights, block_x, preferred_element_type=jnp.float32)
        + reached * jnp.transpose(entry_gain, (1, 2, 0))[..., None]
        + skip_term
    )
    incoming, (z_gate, w_rows) = pass_state(
        device_decay,
        local_final,
        (z_gate, w_out),
        lambda pair: (pair[0], jnp.transpose(pair[1])),
    )
    prefix = jnp.cumprod(
        jnp.concatenate([jnp.ones((head_count, 1), jnp.float32), block_decay[:, :-1]], axis=1),
        axis=1,
    )
    reach_term = jnp.einsum("ctn,hpn->cthp", c_wide, incoming, precision=highest)
    result = (
        result + reach_term * jnp.transpose(entry_gain * prefix[:, :, None], (1, 2, 0))[..., None]
    )
    y_vals = lax.optimization_barrier(result.reshape(row_count, inner_width).astype(jnp.bfloat16))
    gated = y_vals.astype(jnp.float32) * jax.nn.silu(z_gate.astype(jnp.float32))
    group_count = lax.axis_size("tensor")
    squares = jnp.sum(gated * gated, axis=1)
    scaled = (gated * norm_gain[None, :]).astype(jnp.bfloat16)
    out_width = w_rows.shape[0] // group_count
    partial_value = jnp.einsum(
        "tc,gkc->gtk",
        scaled,
        w_rows.reshape(group_count, out_width, inner_width),
        preferred_element_type=jnp.float32,
    ).astype(jnp.bfloat16)
    pad_rows = -(-row_count // out_width)
    square_rows = jnp.pad(squares, (0, pad_rows * out_width - row_count)).reshape(
        pad_rows, out_width
    )
    square_rows = jnp.broadcast_to(
        square_rows.astype(jnp.bfloat16)[None], (group_count, pad_rows, out_width)
    )
    payload = jnp.concatenate([partial_value, square_rows], axis=1)
    summed = lax.psum_scatter(payload, "tensor", scatter_dimension=0, tiled=True)[0]
    total_squares = summed[row_count:].reshape(-1)[:row_count].astype(jnp.float32)
    inv_norm = lax.rsqrt(total_squares / (inner_width * group_count) + 1e-05)
    return (summed[:row_count].astype(jnp.float32) * inv_norm[:, None]).astype(jnp.bfloat16)


def solution(mesh):
    return jax.shard_map(
        local,
        mesh=mesh,
        in_specs=(
            P(("dp", "seq"), "tensor"),
            P(("dp", "seq"), None),
            P(("dp", "seq"), "tensor"),
            P("tensor", ("dp", "seq")),
            P(("dp", "seq")),
            P(None, "tensor"),
            P(),
            P("tensor"),
            P("tensor"),
            P("tensor"),
            P("tensor"),
            P("tensor", None),
        ),
        out_specs=P(("dp", "seq"), "tensor"),
        check_vma=False,
    )
```

```python
import jax
import jax.numpy as jnp
from jax import lax
from jax.sharding import PartitionSpec as P

SPAN = 256


def from_behind(block, axis, distance):
    devices = range(lax.axis_size(axis))
    route = [(i - distance, i) for i in devices if i - distance in devices]
    return lax.ppermute(block, axis, route)


def causal_conv(extended, weights, ext_ids, own_ids, row_count):
    tap_count = weights.shape[0]
    total = jnp.zeros((row_count, extended.shape[1]), jnp.float32)
    for offset in range(tap_count):
        first_row = tap_count - 1 - offset
        window = extended[first_row : first_row + row_count]
        keep_mask = ext_ids[first_row : first_row + row_count] == own_ids
        total = total + jnp.where(
            keep_mask[:, None],
            window.astype(jnp.float32) * weights[offset].astype(jnp.float32),
            0.0,
        )
    return jax.nn.silu(total).astype(jnp.bfloat16)


def with_decay(decay, state):
    head_count = state.shape[0]
    high = decay.astype(jnp.bfloat16)
    low = (decay - high.astype(jnp.float32)).astype(jnp.bfloat16)
    tail_rows = -(-head_count // 16) * 16
    tail = jnp.pad(
        jnp.stack([high, low], 1), ((0, tail_rows - head_count), (0, state.shape[2] - 2))
    )
    flat = state.astype(jnp.bfloat16).reshape(head_count * state.shape[1], state.shape[2])
    return jnp.concatenate([flat, tail], axis=0)


def split_decay(packed, head_count, head_size):
    rows = head_count * head_size
    decay = packed[rows : rows + head_count, 0].astype(jnp.float32) + packed[
        rows : rows + head_count, 1
    ].astype(jnp.float32)
    return decay, packed[:rows].astype(jnp.float32).reshape(head_count, head_size, -1)


def pass_state(device_decay, local_final, passengers, prepare):
    shard_count = lax.axis_size("seq")
    decay, state = device_decay, local_final
    window = 1
    while 4 * window < shard_count - 1:
        sent = with_decay(decay, state)
        if window == 1:
            sent, passengers = lax.optimization_barrier((sent, passengers))
        received = from_behind(sent, "seq", window)
        if window == 1:
            received, passengers = lax.optimization_barrier((received, prepare(passengers)))
        prev_decay, prev_state = split_decay(received, *state.shape[:2])
        state = decay[:, None, None] * prev_state + state
        decay = decay * prev_decay
        window *= 2
    packed = with_decay(decay, state)
    part_count = -(-(shard_count - 1) // window)
    parts = [
        split_decay(from_behind(packed, "seq", 1 + part * window), *state.shape[:2])
        for part in range(part_count)
    ]
    if not parts:
        return jnp.zeros_like(local_final), passengers
    incoming_decay, incoming = parts[0]
    for part_decay, part_state in parts[1:]:
        incoming = incoming_decay[:, None, None] * part_state + incoming
        incoming_decay = incoming_decay * part_decay
    return incoming, passengers


def local(
    x_stream,
    bc_stream,
    z_gate,
    dt_stream,
    doc_ids,
    conv_x,
    conv_bc,
    a_log,
    dt_bias,
    d_skip,
    norm_gain,
    w_out,
):
    highest = lax.Precision.HIGHEST
    row_count = x_stream.shape[0]
    head_count = dt_stream.shape[0]
    inner_width = x_stream.shape[1]
    head_size = inner_width // head_count
    state_size = bc_stream.shape[1] // 2
    tap_count = conv_x.shape[0]
    blocks = row_count // SPAN
    edge_start = row_count - tap_count + 1
    own_ids = doc_ids.astype(jnp.float32)
    x_width = x_stream.shape[1]
    bc_width = bc_stream.shape[1]
    rim = from_behind(
        jnp.concatenate(
            [
                x_stream[edge_start:],
                bc_stream[edge_start:],
                jnp.broadcast_to(own_ids[edge_start:, None], (tap_count - 1, 128)).astype(
                    jnp.bfloat16
                ),
            ],
            axis=1,
        ),
        "seq",
        1,
    )
    rim_x = rim[:, :x_width]
    rim_bc = rim[:, x_width : x_width + bc_width]
    rim_ids = rim[:, x_width + bc_width]
    ext_ids = jnp.concatenate([rim_ids.astype(jnp.float32), own_ids])
    mixed_x = causal_conv(jnp.concatenate([rim_x, x_stream]), conv_x, ext_ids, own_ids, row_count)
    mixed_bc = causal_conv(
        jnp.concatenate([rim_bc, bc_stream]), conv_bc, ext_ids, own_ids, row_count
    )
    prior_id = ext_ids[tap_count - 2]
    step_size = jax.nn.softplus(dt_stream.astype(jnp.float32) + dt_bias[:, None])
    log_rates = -jnp.exp(a_log)[:, None] * step_size
    block_steps = step_size.reshape(head_count, blocks, SPAN)
    cum_rates = jnp.cumsum(log_rates.reshape(head_count, blocks, SPAN), axis=2)
    block_x = mixed_x.reshape(blocks, SPAN, head_count, head_size)
    b_vals = mixed_bc[:, :state_size].reshape(blocks, SPAN, state_size)
    c_vals = mixed_bc[:, state_size:].reshape(blocks, SPAN, state_size)
    c_wide = c_vals.astype(jnp.float32)
    block_ids = own_ids.reshape(blocks, SPAN)
    before = jnp.concatenate([prior_id[None], own_ids[SPAN - 1 :: SPAN][: blocks - 1]])
    carried = block_ids == before[:, None]
    entry_gain = jnp.where(carried[None], jnp.exp(cum_rates), 0.0)
    tail_weight = (
        jnp.where(
            (block_ids == block_ids[:, -1:])[None], jnp.exp(cum_rates[:, :, -1:] - cum_rates), 0.0
        )
        * block_steps
    )
    weighted = block_x.astype(jnp.float32) * jnp.transpose(tail_weight, (1, 2, 0))[..., None]
    block_states = jnp.einsum(
        "cshp,csn->chpn", weighted, b_vals.astype(jnp.float32), precision=highest
    )
    block_decay = jnp.where(carried[:, -1][None], jnp.exp(cum_rates[:, :, -1]), 0.0)
    device_decay = jnp.prod(block_decay, axis=1)
    skip_term = d_skip[None, None, :, None] * block_x.astype(jnp.float32)
    zero_state = jnp.zeros((head_count, head_size, state_size), jnp.float32)
    entry_list = [zero_state]
    for block in range(blocks):
        entry_list.append(block_decay[:, block, None, None] * entry_list[-1] + block_states[block])
    local_final = entry_list[-1]
    local_entries = jnp.stack(entry_list[:-1])
    reached = jnp.einsum("ctn,chpn->cthp", c_wide, local_entries, precision=highest)
    lower_mask = jnp.tril(jnp.ones((SPAN, SPAN), jnp.bool_))
    same_doc = (block_ids[:, :, None] == block_ids[:, None, :]) & lower_mask[None]
    spread = cum_rates[:, :, :, None] - cum_rates[:, :, None, :]
    decay_now = jnp.where(same_doc[None], jnp.exp(jnp.minimum(spread, 0.0)), 0.0)
    scores = jnp.einsum("ctn,csn->cts", c_vals, b_vals, preferred_element_type=jnp.float32)
    weights = (scores[None] * decay_now * block_steps[:, :, None, :]).astype(jnp.bfloat16)
    result = (
        jnp.einsum("hcts,cshp->cthp", weights, block_x, preferred_element_type=jnp.float32)
        + reached * jnp.transpose(entry_gain, (1, 2, 0))[..., None]
        + skip_term
    )
    incoming, (gate_silu, w_rows) = pass_state(
        device_decay,
        local_final,
        (z_gate, w_out),
        lambda pair: (jax.nn.silu(pair[0].astype(jnp.float32)), jnp.transpose(pair[1])),
    )
    prefix = jnp.cumprod(
        jnp.concatenate([jnp.ones((head_count, 1), jnp.float32), block_decay[:, :-1]], axis=1),
        axis=1,
    )
    reach_term = jnp.einsum("ctn,hpn->cthp", c_wide, incoming, precision=highest)
    result = (
        result + reach_term * jnp.transpose(entry_gain * prefix[:, :, None], (1, 2, 0))[..., None]
    )
    y_vals = lax.optimization_barrier(result.reshape(row_count, inner_width).astype(jnp.bfloat16))
    gated = y_vals.astype(jnp.float32) * gate_silu
    group_count = lax.axis_size("tensor")
    squares = jnp.sum(gated * gated, axis=1)
    scaled = (gated * norm_gain[None, :]).astype(jnp.bfloat16)
    out_width = w_rows.shape[0] // group_count
    partial_value = jnp.einsum(
        "tc,gkc->gtk",
        scaled,
        w_rows.reshape(group_count, out_width, inner_width),
        preferred_element_type=jnp.float32,
    ).astype(jnp.bfloat16)
    pad_rows = -(-row_count // out_width)
    square_rows = jnp.pad(squares, (0, pad_rows * out_width - row_count)).reshape(
        pad_rows, out_width
    )
    square_rows = jnp.broadcast_to(
        square_rows.astype(jnp.bfloat16)[None], (group_count, pad_rows, out_width)
    )
    payload = jnp.concatenate([partial_value, square_rows], axis=1)
    summed = lax.psum_scatter(payload, "tensor", scatter_dimension=0, tiled=True)[0]
    total_squares = summed[row_count:].reshape(-1)[:row_count].astype(jnp.float32)
    inv_norm = lax.rsqrt(total_squares / (inner_width * group_count) + 1e-05)
    return (summed[:row_count].astype(jnp.float32) * inv_norm[:, None]).astype(jnp.bfloat16)


def solution(mesh):
    return jax.shard_map(
        local,
        mesh=mesh,
        in_specs=(
            P(("dp", "seq"), "tensor"),
            P(("dp", "seq"), None),
            P(("dp", "seq"), "tensor"),
            P("tensor", ("dp", "seq")),
            P(("dp", "seq")),
            P(None, "tensor"),
            P(),
            P("tensor"),
            P("tensor"),
            P("tensor"),
            P("tensor"),
            P("tensor", None),
        ),
        out_specs=P(("dp", "seq"), "tensor"),
        check_vma=False,
    )
```

```python
import jax
import jax.numpy as jnp
from jax import lax
from jax.sharding import PartitionSpec as P

SPAN = 256


def from_behind(block, axis, distance):
    devices = range(lax.axis_size(axis))
    route = [(i - distance, i) for i in devices if i - distance in devices]
    return lax.ppermute(block, axis, route)


def causal_conv(extended, weights, ext_ids, own_ids, row_count):
    tap_count = weights.shape[0]
    total = jnp.zeros((row_count, extended.shape[1]), jnp.float32)
    for offset in range(tap_count):
        first_row = tap_count - 1 - offset
        window = extended[first_row : first_row + row_count]
        keep_mask = ext_ids[first_row : first_row + row_count] == own_ids
        total = total + jnp.where(
            keep_mask[:, None],
            window.astype(jnp.float32) * weights[offset].astype(jnp.float32),
            0.0,
        )
    return jax.nn.silu(total).astype(jnp.bfloat16)


def with_decay(decay, state):
    head_count = state.shape[0]
    high = decay.astype(jnp.bfloat16)
    low = (decay - high.astype(jnp.float32)).astype(jnp.bfloat16)
    tail_rows = -(-head_count // 16) * 16
    tail = jnp.pad(
        jnp.stack([high, low], 1), ((0, tail_rows - head_count), (0, state.shape[2] - 2))
    )
    flat = state.astype(jnp.bfloat16).reshape(head_count * state.shape[1], state.shape[2])
    return jnp.concatenate([flat, tail], axis=0)


def split_decay(packed, head_count, head_size):
    rows = head_count * head_size
    decay = packed[rows : rows + head_count, 0].astype(jnp.float32) + packed[
        rows : rows + head_count, 1
    ].astype(jnp.float32)
    return decay, packed[:rows].astype(jnp.float32).reshape(head_count, head_size, -1)


def pass_state(device_decay, local_final, passengers, prepare):
    shard_count = lax.axis_size("seq")
    decay, state = device_decay, local_final
    window = 1
    while 4 * window < shard_count - 1:
        sent = with_decay(decay, state)
        if window == 1:
            sent, passengers = lax.optimization_barrier((sent, passengers))
        received = from_behind(sent, "seq", window)
        if window == 1:
            received, passengers = lax.optimization_barrier((received, prepare(passengers)))
        prev_decay, prev_state = split_decay(received, *state.shape[:2])
        state = decay[:, None, None] * prev_state + state
        decay = decay * prev_decay
        window *= 2
    packed = with_decay(decay, state)
    part_count = -(-(shard_count - 1) // window)
    parts = [
        split_decay(from_behind(packed, "seq", 1 + part * window), *state.shape[:2])
        for part in range(part_count)
    ]
    if not parts:
        return jnp.zeros_like(local_final), passengers
    incoming_decay, incoming = parts[0]
    for part_decay, part_state in parts[1:]:
        incoming = incoming_decay[:, None, None] * part_state + incoming
        incoming_decay = incoming_decay * part_decay
    return incoming, passengers


def local(
    x_stream,
    bc_stream,
    z_gate,
    dt_stream,
    doc_ids,
    conv_x,
    conv_bc,
    a_log,
    dt_bias,
    d_skip,
    norm_gain,
    w_out,
):
    highest = lax.Precision.HIGHEST
    row_count = x_stream.shape[0]
    head_count = dt_stream.shape[0]
    inner_width = x_stream.shape[1]
    head_size = inner_width // head_count
    state_size = bc_stream.shape[1] // 2
    tap_count = conv_x.shape[0]
    blocks = row_count // SPAN
    edge_start = row_count - tap_count + 1
    own_ids = doc_ids.astype(jnp.float32)
    x_width = x_stream.shape[1]
    bc_width = bc_stream.shape[1]
    rim = from_behind(
        jnp.concatenate(
            [
                x_stream[edge_start:],
                bc_stream[edge_start:],
                jnp.broadcast_to(own_ids[edge_start:, None], (tap_count - 1, 128)).astype(
                    jnp.bfloat16
                ),
            ],
            axis=1,
        ),
        "seq",
        1,
    )
    rim_x = rim[:, :x_width]
    rim_bc = rim[:, x_width : x_width + bc_width]
    rim_ids = rim[:, x_width + bc_width]
    ext_ids = jnp.concatenate([rim_ids.astype(jnp.float32), own_ids])
    mixed_x = causal_conv(jnp.concatenate([rim_x, x_stream]), conv_x, ext_ids, own_ids, row_count)
    mixed_bc = causal_conv(
        jnp.concatenate([rim_bc, bc_stream]), conv_bc, ext_ids, own_ids, row_count
    )
    prior_id = ext_ids[tap_count - 2]
    step_size = jax.nn.softplus(dt_stream.astype(jnp.float32) + dt_bias[:, None])
    log_rates = -jnp.exp(a_log)[:, None] * step_size
    block_steps = step_size.reshape(head_count, blocks, SPAN)
    cum_rates = jnp.cumsum(log_rates.reshape(head_count, blocks, SPAN), axis=2)
    block_x = mixed_x.reshape(blocks, SPAN, head_count, head_size)
    b_vals = mixed_bc[:, :state_size].reshape(blocks, SPAN, state_size)
    c_vals = mixed_bc[:, state_size:].reshape(blocks, SPAN, state_size)
    c_wide = c_vals.astype(jnp.float32)
    block_ids = own_ids.reshape(blocks, SPAN)
    before = jnp.concatenate([prior_id[None], own_ids[SPAN - 1 :: SPAN][: blocks - 1]])
    carried = block_ids == before[:, None]
    entry_gain = jnp.where(carried[None], jnp.exp(cum_rates), 0.0)
    tail_weight = (
        jnp.where(
            (block_ids == block_ids[:, -1:])[None], jnp.exp(cum_rates[:, :, -1:] - cum_rates), 0.0
        )
        * block_steps
    )
    weighted = block_x.astype(jnp.float32) * jnp.transpose(tail_weight, (1, 2, 0))[..., None]
    block_states = jnp.einsum(
        "cshp,csn->chpn", weighted, b_vals.astype(jnp.float32), precision=highest
    )
    block_decay = jnp.where(carried[:, -1][None], jnp.exp(cum_rates[:, :, -1]), 0.0)
    device_decay = jnp.prod(block_decay, axis=1)
    skip_term = d_skip[None, None, :, None] * block_x.astype(jnp.float32)
    zero_state = jnp.zeros((head_count, head_size, state_size), jnp.float32)
    entry_list = [zero_state]
    for block in range(blocks):
        entry_list.append(block_decay[:, block, None, None] * entry_list[-1] + block_states[block])
    local_final = entry_list[-1]
    local_entries = jnp.stack(entry_list[:-1])
    reached = jnp.einsum("ctn,chpn->cthp", c_wide, local_entries, precision=highest)
    lower_mask = jnp.tril(jnp.ones((SPAN, SPAN), jnp.bool_))
    same_doc = (block_ids[:, :, None] == block_ids[:, None, :]) & lower_mask[None]
    spread = cum_rates[:, :, :, None] - cum_rates[:, :, None, :]
    decay_now = jnp.where(same_doc[None], jnp.exp(jnp.minimum(spread, 0.0)), 0.0)
    scores = jnp.einsum("ctn,csn->cts", c_vals, b_vals, preferred_element_type=jnp.float32)
    weights = (scores[None] * decay_now * block_steps[:, :, None, :]).astype(jnp.bfloat16)
    result = (
        jnp.einsum("hcts,cshp->cthp", weights, block_x, preferred_element_type=jnp.float32)
        + reached * jnp.transpose(entry_gain, (1, 2, 0))[..., None]
        + skip_term
    )
    incoming, (gate_silu, w_rows) = pass_state(
        device_decay,
        local_final,
        (z_gate, w_out),
        lambda pair: (jax.nn.silu(pair[0].astype(jnp.float32)), jnp.transpose(pair[1])),
    )
    prefix = jnp.cumprod(
        jnp.concatenate([jnp.ones((head_count, 1), jnp.float32), block_decay[:, :-1]], axis=1),
        axis=1,
    )
    reach_term = jnp.einsum("ctn,hpn->cthp", c_wide, incoming, precision=highest)
    result = (
        result + reach_term * jnp.transpose(entry_gain * prefix[:, :, None], (1, 2, 0))[..., None]
    )
    y_vals = lax.optimization_barrier(result.reshape(row_count, inner_width).astype(jnp.bfloat16))
    gated = y_vals.astype(jnp.float32) * gate_silu
    group_count = lax.axis_size("tensor")
    squares = jnp.sum(gated * gated, axis=1)
    scaled = (gated * norm_gain[None, :]).astype(jnp.bfloat16)
    out_width = w_rows.shape[0] // group_count
    partial_value = jnp.einsum(
        "tc,gkc->gtk",
        scaled,
        w_rows.reshape(group_count, out_width, inner_width),
        preferred_element_type=jnp.float32,
    ).astype(jnp.bfloat16)
    square_column = jnp.broadcast_to(
        squares.astype(jnp.bfloat16)[None, :, None], (group_count, row_count, 1)
    )
    payload = jnp.concatenate([partial_value, square_column], axis=2)
    summed = lax.psum_scatter(payload, "tensor", scatter_dimension=0, tiled=True)[0]
    total_squares = summed[:, out_width].astype(jnp.float32)
    inv_norm = lax.rsqrt(total_squares / (inner_width * group_count) + 1e-05)
    return (summed[:, :out_width].astype(jnp.float32) * inv_norm[:, None]).astype(jnp.bfloat16)


def solution(mesh):
    return jax.shard_map(
        local,
        mesh=mesh,
        in_specs=(
            P(("dp", "seq"), "tensor"),
            P(("dp", "seq"), None),
            P(("dp", "seq"), "tensor"),
            P("tensor", ("dp", "seq")),
            P(("dp", "seq")),
            P(None, "tensor"),
            P(),
            P("tensor"),
            P("tensor"),
            P("tensor"),
            P("tensor"),
            P("tensor", None),
        ),
        out_specs=P(("dp", "seq"), "tensor"),
        check_vma=False,
    )
```

```python
import jax
import jax.numpy as jnp
from jax import lax
from jax.sharding import PartitionSpec as P

SPAN = 256


def from_behind(block, axis, distance):
    devices = range(lax.axis_size(axis))
    route = [(i - distance, i) for i in devices if i - distance in devices]
    return lax.ppermute(block, axis, route)


def causal_conv(extended, weights, ext_ids, own_ids, row_count):
    tap_count = weights.shape[0]
    total = jnp.zeros((row_count, extended.shape[1]), jnp.float32)
    for offset in range(tap_count):
        first_row = tap_count - 1 - offset
        window = extended[first_row : first_row + row_count]
        keep_mask = ext_ids[first_row : first_row + row_count] == own_ids
        total = total + jnp.where(
            keep_mask[:, None],
            window.astype(jnp.float32) * weights[offset].astype(jnp.float32),
            0.0,
        )
    return jax.nn.silu(total).astype(jnp.bfloat16)


def with_decay(decay, state):
    head_count = state.shape[0]
    high = decay.astype(jnp.bfloat16)
    low = (decay - high.astype(jnp.float32)).astype(jnp.bfloat16)
    tail_rows = -(-head_count // 16) * 16
    tail = jnp.pad(
        jnp.stack([high, low], 1), ((0, tail_rows - head_count), (0, state.shape[2] - 2))
    )
    flat = state.astype(jnp.bfloat16).reshape(head_count * state.shape[1], state.shape[2])
    return jnp.concatenate([flat, tail], axis=0)


def split_decay(packed, head_count, head_size):
    rows = head_count * head_size
    decay = packed[rows : rows + head_count, 0].astype(jnp.float32) + packed[
        rows : rows + head_count, 1
    ].astype(jnp.float32)
    return decay, packed[:rows].astype(jnp.float32).reshape(head_count, head_size, -1)


def pass_state(device_decay, local_final, passengers, prepare):
    shard_count = lax.axis_size("seq")
    decay, state = device_decay, local_final
    window = 1
    while 4 * window < shard_count - 1:
        sent = with_decay(decay, state)
        if window == 1:
            sent, passengers = lax.optimization_barrier((sent, passengers))
        received = from_behind(sent, "seq", window)
        if window == 1:
            received, passengers = lax.optimization_barrier((received, prepare(passengers)))
        prev_decay, prev_state = split_decay(received, *state.shape[:2])
        state = decay[:, None, None] * prev_state + state
        decay = decay * prev_decay
        window *= 2
    packed = with_decay(decay, state)
    part_count = -(-(shard_count - 1) // window)
    parts = [
        split_decay(from_behind(packed, "seq", 1 + part * window), *state.shape[:2])
        for part in range(part_count)
    ]
    if not parts:
        return jnp.zeros_like(local_final), passengers
    incoming_decay, incoming = parts[0]
    for part_decay, part_state in parts[1:]:
        incoming = incoming_decay[:, None, None] * part_state + incoming
        incoming_decay = incoming_decay * part_decay
    return incoming, passengers


def local(
    x_stream,
    bc_stream,
    z_gate,
    dt_stream,
    doc_ids,
    conv_x,
    conv_bc,
    a_log,
    dt_bias,
    d_skip,
    norm_gain,
    w_out,
):
    highest = lax.Precision.HIGHEST
    row_count = x_stream.shape[0]
    head_count = dt_stream.shape[0]
    inner_width = x_stream.shape[1]
    head_size = inner_width // head_count
    state_size = bc_stream.shape[1] // 2
    tap_count = conv_x.shape[0]
    blocks = row_count // SPAN
    edge_start = row_count - tap_count + 1
    own_ids = doc_ids.astype(jnp.float32)
    x_width = x_stream.shape[1]
    bc_width = bc_stream.shape[1]
    rim = from_behind(
        jnp.concatenate(
            [
                x_stream[edge_start:],
                bc_stream[edge_start:],
                jnp.broadcast_to(own_ids[edge_start:, None], (tap_count - 1, 128)).astype(
                    jnp.bfloat16
                ),
            ],
            axis=1,
        ),
        "seq",
        1,
    )
    rim_x = rim[:, :x_width]
    rim_bc = rim[:, x_width : x_width + bc_width]
    rim_ids = rim[:, x_width + bc_width]
    ext_ids = jnp.concatenate([rim_ids.astype(jnp.float32), own_ids])
    mixed_x = causal_conv(jnp.concatenate([rim_x, x_stream]), conv_x, ext_ids, own_ids, row_count)
    mixed_bc = causal_conv(
        jnp.concatenate([rim_bc, bc_stream]), conv_bc, ext_ids, own_ids, row_count
    )
    prior_id = ext_ids[tap_count - 2]
    step_size = jax.nn.softplus(dt_stream.astype(jnp.float32) + dt_bias[:, None])
    log_rates = -jnp.exp(a_log)[:, None] * step_size
    block_steps = step_size.reshape(head_count, blocks, SPAN)
    cum_rates = jnp.cumsum(log_rates.reshape(head_count, blocks, SPAN), axis=2)
    block_x = mixed_x.reshape(blocks, SPAN, head_count, head_size)
    b_vals = mixed_bc[:, :state_size].reshape(blocks, SPAN, state_size)
    c_vals = mixed_bc[:, state_size:].reshape(blocks, SPAN, state_size)
    c_wide = c_vals.astype(jnp.float32)
    block_ids = own_ids.reshape(blocks, SPAN)
    before = jnp.concatenate([prior_id[None], own_ids[SPAN - 1 :: SPAN][: blocks - 1]])
    carried = block_ids == before[:, None]
    entry_gain = jnp.where(carried[None], jnp.exp(cum_rates), 0.0)
    tail_weight = (
        jnp.where(
            (block_ids == block_ids[:, -1:])[None], jnp.exp(cum_rates[:, :, -1:] - cum_rates), 0.0
        )
        * block_steps
    )
    weighted = block_x.astype(jnp.float32) * jnp.transpose(tail_weight, (1, 2, 0))[..., None]
    block_states = jnp.einsum(
        "cshp,csn->chpn", weighted, b_vals.astype(jnp.float32), precision=highest
    )
    block_decay = jnp.where(carried[:, -1][None], jnp.exp(cum_rates[:, :, -1]), 0.0)
    device_decay = jnp.prod(block_decay, axis=1)
    skip_term = d_skip[None, None, :, None] * block_x.astype(jnp.float32)
    zero_state = jnp.zeros((head_count, head_size, state_size), jnp.float32)
    entry_list = [zero_state]
    for block in range(blocks):
        entry_list.append(block_decay[:, block, None, None] * entry_list[-1] + block_states[block])
    local_final = entry_list[-1]
    local_entries = jnp.stack(entry_list[:-1])
    reached = jnp.einsum("ctn,chpn->cthp", c_wide, local_entries, precision=highest)
    lower_mask = jnp.tril(jnp.ones((SPAN, SPAN), jnp.bool_))
    same_doc = (block_ids[:, :, None] == block_ids[:, None, :]) & lower_mask[None]
    spread = cum_rates[:, :, :, None] - cum_rates[:, :, None, :]
    decay_now = jnp.where(same_doc[None], jnp.exp(jnp.minimum(spread, 0.0)), 0.0)
    scores = jnp.einsum("ctn,csn->cts", c_vals, b_vals, preferred_element_type=jnp.float32)
    weights = (scores[None] * decay_now * block_steps[:, :, None, :]).astype(jnp.bfloat16)
    result = (
        jnp.einsum("hcts,cshp->cthp", weights, block_x, preferred_element_type=jnp.float32)
        + reached * jnp.transpose(entry_gain, (1, 2, 0))[..., None]
        + skip_term
    )
    incoming, (gate_silu, w_rows) = pass_state(
        device_decay,
        local_final,
        (z_gate, w_out),
        lambda pair: (jax.nn.silu(pair[0].astype(jnp.float32)), jnp.transpose(pair[1])),
    )
    prefix = jnp.cumprod(
        jnp.concatenate([jnp.ones((head_count, 1), jnp.float32), block_decay[:, :-1]], axis=1),
        axis=1,
    )
    reach_term = jnp.einsum("ctn,hpn->cthp", c_wide, incoming, precision=highest)
    result = (
        result + reach_term * jnp.transpose(entry_gain * prefix[:, :, None], (1, 2, 0))[..., None]
    )
    y_vals = result.reshape(row_count, inner_width).astype(jnp.bfloat16)
    gated = y_vals.astype(jnp.float32) * gate_silu
    group_count = lax.axis_size("tensor")
    squares = jnp.sum(gated * gated, axis=1)
    scaled = (gated * norm_gain[None, :]).astype(jnp.bfloat16)
    out_width = w_rows.shape[0] // group_count
    partial_value = jnp.einsum(
        "tc,gkc->gtk",
        scaled,
        w_rows.reshape(group_count, out_width, inner_width),
        preferred_element_type=jnp.float32,
    ).astype(jnp.bfloat16)
    square_column = jnp.broadcast_to(
        squares.astype(jnp.bfloat16)[None, :, None], (group_count, row_count, 1)
    )
    payload = jnp.concatenate([partial_value, square_column], axis=2)
    summed = lax.psum_scatter(payload, "tensor", scatter_dimension=0, tiled=True)[0]
    total_squares = summed[:, out_width].astype(jnp.float32)
    inv_norm = lax.rsqrt(total_squares / (inner_width * group_count) + 1e-05)
    return (summed[:, :out_width].astype(jnp.float32) * inv_norm[:, None]).astype(jnp.bfloat16)


def solution(mesh):
    return jax.shard_map(
        local,
        mesh=mesh,
        in_specs=(
            P(("dp", "seq"), "tensor"),
            P(("dp", "seq"), None),
            P(("dp", "seq"), "tensor"),
            P("tensor", ("dp", "seq")),
            P(("dp", "seq")),
            P(None, "tensor"),
            P(),
            P("tensor"),
            P("tensor"),
            P("tensor"),
            P("tensor"),
            P("tensor", None),
        ),
        out_specs=P(("dp", "seq"), "tensor"),
        check_vma=False,
    )
```

```python
import jax
import jax.numpy as jnp
from jax import lax
from jax.sharding import PartitionSpec as P

SPAN = 256


def from_behind(block, axis, distance):
    devices = range(lax.axis_size(axis))
    route = [(i - distance, i) for i in devices if i - distance in devices]
    return lax.ppermute(block, axis, route)


def causal_conv(extended, weights, ext_ids, own_ids, row_count):
    tap_count = weights.shape[0]
    total = jnp.zeros((row_count, extended.shape[1]), jnp.float32)
    for offset in range(tap_count):
        first_row = tap_count - 1 - offset
        window = extended[first_row : first_row + row_count]
        keep_mask = ext_ids[first_row : first_row + row_count] == own_ids
        total = total + jnp.where(
            keep_mask[:, None],
            window.astype(jnp.float32) * weights[offset].astype(jnp.float32),
            0.0,
        )
    return jax.nn.silu(total).astype(jnp.bfloat16)


def with_decay(decay, state):
    head_count = state.shape[0]
    high = decay.astype(jnp.bfloat16)
    low = (decay - high.astype(jnp.float32)).astype(jnp.bfloat16)
    tail_rows = -(-head_count // 16) * 16
    tail = jnp.pad(
        jnp.stack([high, low], 1), ((0, tail_rows - head_count), (0, state.shape[2] - 2))
    )
    flat = state.astype(jnp.bfloat16).reshape(head_count * state.shape[1], state.shape[2])
    return jnp.concatenate([flat, tail], axis=0)


def split_decay(packed, head_count, head_size):
    rows = head_count * head_size
    decay = packed[rows : rows + head_count, 0].astype(jnp.float32) + packed[
        rows : rows + head_count, 1
    ].astype(jnp.float32)
    return decay, packed[:rows].astype(jnp.float32).reshape(head_count, head_size, -1)


def pass_state(device_decay, local_final, passengers, prepare):
    shard_count = lax.axis_size("seq")
    decay, state = device_decay, local_final
    window = 1
    while 4 * window < shard_count - 1:
        sent = with_decay(decay, state)
        if window in prepare:
            sent, passengers = lax.optimization_barrier((sent, passengers))
        received = from_behind(sent, "seq", window)
        if window in prepare:
            received, passengers = lax.optimization_barrier(
                (received, prepare[window](passengers))
            )
        prev_decay, prev_state = split_decay(received, *state.shape[:2])
        state = decay[:, None, None] * prev_state + state
        decay = decay * prev_decay
        window *= 2
    packed = with_decay(decay, state)
    part_count = -(-(shard_count - 1) // window)
    parts = [
        split_decay(from_behind(packed, "seq", 1 + part * window), *state.shape[:2])
        for part in range(part_count)
    ]
    if not parts:
        return jnp.zeros_like(local_final), passengers
    incoming_decay, incoming = parts[0]
    for part_decay, part_state in parts[1:]:
        incoming = incoming_decay[:, None, None] * part_state + incoming
        incoming_decay = incoming_decay * part_decay
    return incoming, passengers


def local(
    x_stream,
    bc_stream,
    z_gate,
    dt_stream,
    doc_ids,
    conv_x,
    conv_bc,
    a_log,
    dt_bias,
    d_skip,
    norm_gain,
    w_out,
):
    highest = lax.Precision.HIGHEST
    row_count = x_stream.shape[0]
    head_count = dt_stream.shape[0]
    inner_width = x_stream.shape[1]
    head_size = inner_width // head_count
    state_size = bc_stream.shape[1] // 2
    tap_count = conv_x.shape[0]
    blocks = row_count // SPAN
    edge_start = row_count - tap_count + 1
    own_ids = doc_ids.astype(jnp.float32)
    x_width = x_stream.shape[1]
    bc_width = bc_stream.shape[1]
    rim = from_behind(
        jnp.concatenate(
            [
                x_stream[edge_start:],
                bc_stream[edge_start:],
                jnp.broadcast_to(own_ids[edge_start:, None], (tap_count - 1, 128)).astype(
                    jnp.bfloat16
                ),
            ],
            axis=1,
        ),
        "seq",
        1,
    )
    rim_x = rim[:, :x_width]
    rim_bc = rim[:, x_width : x_width + bc_width]
    rim_ids = rim[:, x_width + bc_width]
    ext_ids = jnp.concatenate([rim_ids.astype(jnp.float32), own_ids])
    mixed_x = causal_conv(jnp.concatenate([rim_x, x_stream]), conv_x, ext_ids, own_ids, row_count)
    mixed_bc = causal_conv(
        jnp.concatenate([rim_bc, bc_stream]), conv_bc, ext_ids, own_ids, row_count
    )
    prior_id = ext_ids[tap_count - 2]
    step_size = jax.nn.softplus(dt_stream.astype(jnp.float32) + dt_bias[:, None])
    log_rates = -jnp.exp(a_log)[:, None] * step_size
    block_steps = step_size.reshape(head_count, blocks, SPAN)
    cum_rates = jnp.cumsum(log_rates.reshape(head_count, blocks, SPAN), axis=2)
    block_x = mixed_x.reshape(blocks, SPAN, head_count, head_size)
    b_vals = mixed_bc[:, :state_size].reshape(blocks, SPAN, state_size)
    c_vals = mixed_bc[:, state_size:].reshape(blocks, SPAN, state_size)
    c_wide = c_vals.astype(jnp.float32)
    block_ids = own_ids.reshape(blocks, SPAN)
    before = jnp.concatenate([prior_id[None], own_ids[SPAN - 1 :: SPAN][: blocks - 1]])
    carried = block_ids == before[:, None]
    entry_gain = jnp.where(carried[None], jnp.exp(cum_rates), 0.0)
    tail_weight = (
        jnp.where(
            (block_ids == block_ids[:, -1:])[None], jnp.exp(cum_rates[:, :, -1:] - cum_rates), 0.0
        )
        * block_steps
    )
    weighted = block_x.astype(jnp.float32) * jnp.transpose(tail_weight, (1, 2, 0))[..., None]
    block_states = jnp.einsum(
        "cshp,csn->chpn", weighted, b_vals.astype(jnp.float32), precision=highest
    )
    block_decay = jnp.where(carried[:, -1][None], jnp.exp(cum_rates[:, :, -1]), 0.0)
    device_decay = jnp.prod(block_decay, axis=1)
    skip_term = d_skip[None, None, :, None] * block_x.astype(jnp.float32)
    zero_state = jnp.zeros((head_count, head_size, state_size), jnp.float32)
    entry_list = [zero_state]
    for block in range(blocks):
        entry_list.append(block_decay[:, block, None, None] * entry_list[-1] + block_states[block])
    local_final = entry_list[-1]
    local_entries = jnp.stack(entry_list[:-1])
    reached = jnp.einsum("ctn,chpn->cthp", c_wide, local_entries, precision=highest)
    lower_mask = jnp.tril(jnp.ones((SPAN, SPAN), jnp.bool_))
    same_doc = (block_ids[:, :, None] == block_ids[:, None, :]) & lower_mask[None]
    spread = cum_rates[:, :, :, None] - cum_rates[:, :, None, :]
    decay_now = jnp.where(same_doc[None], jnp.exp(jnp.minimum(spread, 0.0)), 0.0)
    scores = jnp.einsum("ctn,csn->cts", c_vals, b_vals, preferred_element_type=jnp.float32)
    weights = (scores[None] * decay_now * block_steps[:, :, None, :]).astype(jnp.bfloat16)
    result = (
        jnp.einsum("hcts,cshp->cthp", weights, block_x, preferred_element_type=jnp.float32)
        + reached * jnp.transpose(entry_gain, (1, 2, 0))[..., None]
        + skip_term
    )
    incoming, (gate_silu, w_rows) = pass_state(
        device_decay,
        local_final,
        (z_gate, w_out),
        {
            1: lambda pair: (jax.nn.silu(pair[0].astype(jnp.float32)), pair[1]),
            2: lambda pair: (pair[0], jnp.transpose(pair[1])),
        },
    )
    prefix = jnp.cumprod(
        jnp.concatenate([jnp.ones((head_count, 1), jnp.float32), block_decay[:, :-1]], axis=1),
        axis=1,
    )
    reach_term = jnp.einsum("ctn,hpn->cthp", c_wide, incoming, precision=highest)
    result = (
        result + reach_term * jnp.transpose(entry_gain * prefix[:, :, None], (1, 2, 0))[..., None]
    )
    y_vals = result.reshape(row_count, inner_width).astype(jnp.bfloat16)
    gated = y_vals.astype(jnp.float32) * gate_silu
    group_count = lax.axis_size("tensor")
    squares = jnp.sum(gated * gated, axis=1)
    scaled = (gated * norm_gain[None, :]).astype(jnp.bfloat16)
    out_width = w_rows.shape[0] // group_count
    partial_value = jnp.einsum(
        "tc,gkc->gtk",
        scaled,
        w_rows.reshape(group_count, out_width, inner_width),
        preferred_element_type=jnp.float32,
    ).astype(jnp.bfloat16)
    square_column = jnp.broadcast_to(
        squares.astype(jnp.bfloat16)[None, :, None], (group_count, row_count, 1)
    )
    payload = jnp.concatenate([partial_value, square_column], axis=2)
    summed = lax.psum_scatter(payload, "tensor", scatter_dimension=0, tiled=True)[0]
    total_squares = summed[:, out_width].astype(jnp.float32)
    inv_norm = lax.rsqrt(total_squares / (inner_width * group_count) + 1e-05)
    return (summed[:, :out_width].astype(jnp.float32) * inv_norm[:, None]).astype(jnp.bfloat16)


def solution(mesh):
    return jax.shard_map(
        local,
        mesh=mesh,
        in_specs=(
            P(("dp", "seq"), "tensor"),
            P(("dp", "seq"), None),
            P(("dp", "seq"), "tensor"),
            P("tensor", ("dp", "seq")),
            P(("dp", "seq")),
            P(None, "tensor"),
            P(),
            P("tensor"),
            P("tensor"),
            P("tensor"),
            P("tensor"),
            P("tensor", None),
        ),
        out_specs=P(("dp", "seq"), "tensor"),
        check_vma=False,
    )
```

```python
import jax
import jax.numpy as jnp
from jax import lax
from jax.sharding import PartitionSpec as P

SPAN = 256


def from_behind(block, axis, distance):
    devices = range(lax.axis_size(axis))
    route = [(i - distance, i) for i in devices if i - distance in devices]
    return lax.ppermute(block, axis, route)


def causal_conv(extended, weights, ext_ids, own_ids, row_count):
    tap_count = weights.shape[0]
    total = jnp.zeros((row_count, extended.shape[1]), jnp.float32)
    for offset in range(tap_count):
        first_row = tap_count - 1 - offset
        window = extended[first_row : first_row + row_count]
        keep_mask = ext_ids[first_row : first_row + row_count] == own_ids
        total = total + jnp.where(
            keep_mask[:, None],
            window.astype(jnp.float32) * weights[offset].astype(jnp.float32),
            0.0,
        )
    return jax.nn.silu(total).astype(jnp.bfloat16)


def with_decay(decay, state):
    head_count = state.shape[0]
    high = decay.astype(jnp.bfloat16)
    low = (decay - high.astype(jnp.float32)).astype(jnp.bfloat16)
    tail_rows = -(-head_count // 16) * 16
    tail = jnp.pad(
        jnp.stack([high, low], 1), ((0, tail_rows - head_count), (0, state.shape[2] - 2))
    )
    flat = state.astype(jnp.bfloat16).reshape(head_count * state.shape[1], state.shape[2])
    return jnp.concatenate([flat, tail], axis=0)


def split_decay(packed, head_count, head_size):
    rows = head_count * head_size
    decay = packed[rows : rows + head_count, 0].astype(jnp.float32) + packed[
        rows : rows + head_count, 1
    ].astype(jnp.float32)
    return decay, packed[:rows].astype(jnp.float32).reshape(head_count, head_size, -1)


def pass_state(device_decay, local_final, passengers, prepare):
    shard_count = lax.axis_size("seq")
    decay, state = device_decay, local_final
    window = 1
    while 4 * window < shard_count - 1:
        sent = with_decay(decay, state)
        if window == 1:
            sent, passengers = lax.optimization_barrier((sent, passengers))
        received = from_behind(sent, "seq", window)
        if window == 1:
            received, passengers = lax.optimization_barrier((received, prepare(passengers)))
        prev_decay, prev_state = split_decay(received, *state.shape[:2])
        state = decay[:, None, None] * prev_state + state
        decay = decay * prev_decay
        window *= 2
    packed = with_decay(decay, state)
    part_count = -(-(shard_count - 1) // window)
    parts = [
        split_decay(from_behind(packed, "seq", 1 + part * window), *state.shape[:2])
        for part in range(part_count)
    ]
    if not parts:
        return jnp.zeros_like(local_final), passengers
    incoming_decay, incoming = parts[0]
    for part_decay, part_state in parts[1:]:
        incoming = incoming_decay[:, None, None] * part_state + incoming
        incoming_decay = incoming_decay * part_decay
    return incoming, passengers


def local(
    x_stream,
    bc_stream,
    z_gate,
    dt_stream,
    doc_ids,
    conv_x,
    conv_bc,
    a_log,
    dt_bias,
    d_skip,
    norm_gain,
    w_out,
):
    highest = lax.Precision.HIGHEST
    row_count = x_stream.shape[0]
    head_count = dt_stream.shape[0]
    inner_width = x_stream.shape[1]
    head_size = inner_width // head_count
    state_size = bc_stream.shape[1] // 2
    tap_count = conv_x.shape[0]
    blocks = row_count // SPAN
    edge_start = row_count - tap_count + 1
    own_ids = doc_ids.astype(jnp.float32)
    x_width = x_stream.shape[1]
    bc_width = bc_stream.shape[1]
    rim = from_behind(
        jnp.concatenate(
            [
                x_stream[edge_start:],
                bc_stream[edge_start:],
                jnp.broadcast_to(own_ids[edge_start:, None], (tap_count - 1, 128)).astype(
                    jnp.bfloat16
                ),
            ],
            axis=1,
        ),
        "seq",
        1,
    )
    rim_x = rim[:, :x_width]
    rim_bc = rim[:, x_width : x_width + bc_width]
    rim_ids = rim[:, x_width + bc_width]
    ext_ids = jnp.concatenate([rim_ids.astype(jnp.float32), own_ids])
    mixed_x = causal_conv(jnp.concatenate([rim_x, x_stream]), conv_x, ext_ids, own_ids, row_count)
    mixed_bc = causal_conv(
        jnp.concatenate([rim_bc, bc_stream]), conv_bc, ext_ids, own_ids, row_count
    )
    prior_id = ext_ids[tap_count - 2]
    step_size = jax.nn.softplus(dt_stream.astype(jnp.float32) + dt_bias[:, None])
    log_rates = -jnp.exp(a_log)[:, None] * step_size
    block_steps = step_size.reshape(head_count, blocks, SPAN)
    running = jnp.triu(jnp.ones((SPAN, SPAN), jnp.float32))
    cum_rates = jnp.einsum(
        "hcs,su->hcu",
        log_rates.reshape(head_count, blocks, SPAN),
        running,
        precision=lax.Precision.HIGHEST,
    )
    block_x = mixed_x.reshape(blocks, SPAN, head_count, head_size)
    b_vals = mixed_bc[:, :state_size].reshape(blocks, SPAN, state_size)
    c_vals = mixed_bc[:, state_size:].reshape(blocks, SPAN, state_size)
    c_wide = c_vals.astype(jnp.float32)
    block_ids = own_ids.reshape(blocks, SPAN)
    before = jnp.concatenate([prior_id[None], own_ids[SPAN - 1 :: SPAN][: blocks - 1]])
    carried = block_ids == before[:, None]
    entry_gain = jnp.where(carried[None], jnp.exp(cum_rates), 0.0)
    tail_weight = (
        jnp.where(
            (block_ids == block_ids[:, -1:])[None], jnp.exp(cum_rates[:, :, -1:] - cum_rates), 0.0
        )
        * block_steps
    )
    weighted = block_x.astype(jnp.float32) * jnp.transpose(tail_weight, (1, 2, 0))[..., None]
    block_states = jnp.einsum(
        "cshp,csn->chpn", weighted, b_vals.astype(jnp.float32), precision=highest
    )
    block_decay = jnp.where(carried[:, -1][None], jnp.exp(cum_rates[:, :, -1]), 0.0)
    device_decay = jnp.prod(block_decay, axis=1)
    skip_term = d_skip[None, None, :, None] * block_x.astype(jnp.float32)
    zero_state = jnp.zeros((head_count, head_size, state_size), jnp.float32)
    entry_list = [zero_state]
    for block in range(blocks):
        entry_list.append(block_decay[:, block, None, None] * entry_list[-1] + block_states[block])
    local_final = entry_list[-1]
    local_entries = jnp.stack(entry_list[:-1])
    reached = jnp.einsum("ctn,chpn->cthp", c_wide, local_entries, precision=highest)
    lower_mask = jnp.tril(jnp.ones((SPAN, SPAN), jnp.bool_))
    same_doc = (block_ids[:, :, None] == block_ids[:, None, :]) & lower_mask[None]
    spread = cum_rates[:, :, :, None] - cum_rates[:, :, None, :]
    decay_now = jnp.where(same_doc[None], jnp.exp(jnp.minimum(spread, 0.0)), 0.0)
    scores = jnp.einsum("ctn,csn->cts", c_vals, b_vals, preferred_element_type=jnp.float32)
    weights = (scores[None] * decay_now * block_steps[:, :, None, :]).astype(jnp.bfloat16)
    result = (
        jnp.einsum("hcts,cshp->cthp", weights, block_x, preferred_element_type=jnp.float32)
        + reached * jnp.transpose(entry_gain, (1, 2, 0))[..., None]
        + skip_term
    )
    incoming, (gate_silu, w_rows) = pass_state(
        device_decay,
        local_final,
        (z_gate, w_out),
        lambda pair: (jax.nn.silu(pair[0].astype(jnp.float32)), jnp.transpose(pair[1])),
    )
    prefix = jnp.cumprod(
        jnp.concatenate([jnp.ones((head_count, 1), jnp.float32), block_decay[:, :-1]], axis=1),
        axis=1,
    )
    reach_term = jnp.einsum("ctn,hpn->cthp", c_wide, incoming, precision=highest)
    result = (
        result + reach_term * jnp.transpose(entry_gain * prefix[:, :, None], (1, 2, 0))[..., None]
    )
    y_vals = result.reshape(row_count, inner_width).astype(jnp.bfloat16)
    gated = y_vals.astype(jnp.float32) * gate_silu
    group_count = lax.axis_size("tensor")
    squares = jnp.sum(gated * gated, axis=1)
    scaled = (gated * norm_gain[None, :]).astype(jnp.bfloat16)
    out_width = w_rows.shape[0] // group_count
    partial_value = jnp.einsum(
        "tc,gkc->gtk",
        scaled,
        w_rows.reshape(group_count, out_width, inner_width),
        preferred_element_type=jnp.float32,
    ).astype(jnp.bfloat16)
    square_column = jnp.broadcast_to(
        squares.astype(jnp.bfloat16)[None, :, None], (group_count, row_count, 1)
    )
    payload = jnp.concatenate([partial_value, square_column], axis=2)
    summed = lax.psum_scatter(payload, "tensor", scatter_dimension=0, tiled=True)[0]
    total_squares = summed[:, out_width].astype(jnp.float32)
    inv_norm = lax.rsqrt(total_squares / (inner_width * group_count) + 1e-05)
    return (summed[:, :out_width].astype(jnp.float32) * inv_norm[:, None]).astype(jnp.bfloat16)


def solution(mesh):
    return jax.shard_map(
        local,
        mesh=mesh,
        in_specs=(
            P(("dp", "seq"), "tensor"),
            P(("dp", "seq"), None),
            P(("dp", "seq"), "tensor"),
            P("tensor", ("dp", "seq")),
            P(("dp", "seq")),
            P(None, "tensor"),
            P(),
            P("tensor"),
            P("tensor"),
            P("tensor"),
            P("tensor"),
            P("tensor", None),
        ),
        out_specs=P(("dp", "seq"), "tensor"),
        check_vma=False,
    )
```

```python
import jax
import jax.numpy as jnp
from jax import lax
from jax.sharding import PartitionSpec as P

SPAN = 256


def from_behind(block, axis, distance):
    devices = range(lax.axis_size(axis))
    route = [(i - distance, i) for i in devices if i - distance in devices]
    return lax.ppermute(block, axis, route)


def causal_conv(extended, weights, ext_ids, own_ids, row_count):
    tap_count = weights.shape[0]
    total = jnp.zeros((row_count, extended.shape[1]), jnp.float32)
    for offset in range(tap_count):
        first_row = tap_count - 1 - offset
        window = extended[first_row : first_row + row_count]
        keep_mask = ext_ids[first_row : first_row + row_count] == own_ids
        total = total + jnp.where(
            keep_mask[:, None],
            window.astype(jnp.float32) * weights[offset].astype(jnp.float32),
            0.0,
        )
    return jax.nn.silu(total).astype(jnp.bfloat16)


def with_decay(decay, state):
    head_count = state.shape[0]
    high = decay.astype(jnp.bfloat16)
    low = (decay - high.astype(jnp.float32)).astype(jnp.bfloat16)
    tail_rows = -(-head_count // 16) * 16
    tail = jnp.pad(
        jnp.stack([high, low], 1), ((0, tail_rows - head_count), (0, state.shape[2] - 2))
    )
    flat = state.astype(jnp.bfloat16).reshape(head_count * state.shape[1], state.shape[2])
    return jnp.concatenate([flat, tail], axis=0)


def split_decay(packed, head_count, head_size):
    rows = head_count * head_size
    decay = packed[rows : rows + head_count, 0].astype(jnp.float32) + packed[
        rows : rows + head_count, 1
    ].astype(jnp.float32)
    return decay, packed[:rows].astype(jnp.float32).reshape(head_count, head_size, -1)


def pass_state(device_decay, local_final, passengers, prepare):
    shard_count = lax.axis_size("seq")
    decay, state = device_decay, local_final
    window = 1
    while 4 * window < shard_count - 1:
        sent = with_decay(decay, state)
        if window == 1:
            sent, passengers = lax.optimization_barrier((sent, passengers))
        received = from_behind(sent, "seq", window)
        if window == 1:
            received, passengers = lax.optimization_barrier((received, prepare(passengers)))
        prev_decay, prev_state = split_decay(received, *state.shape[:2])
        state = decay[:, None, None] * prev_state + state
        decay = decay * prev_decay
        window *= 2
    packed = with_decay(decay, state)
    part_count = -(-(shard_count - 1) // window)
    parts = [
        split_decay(from_behind(packed, "seq", 1 + part * window), *state.shape[:2])
        for part in range(part_count)
    ]
    if not parts:
        return jnp.zeros_like(local_final), passengers
    incoming_decay, incoming = parts[0]
    for part_decay, part_state in parts[1:]:
        incoming = incoming_decay[:, None, None] * part_state + incoming
        incoming_decay = incoming_decay * part_decay
    return incoming, passengers


def local(
    x_stream,
    bc_stream,
    z_gate,
    dt_stream,
    doc_ids,
    conv_x,
    conv_bc,
    a_log,
    dt_bias,
    d_skip,
    norm_gain,
    w_out,
):
    highest = lax.Precision.HIGHEST
    row_count = x_stream.shape[0]
    head_count = dt_stream.shape[0]
    inner_width = x_stream.shape[1]
    head_size = inner_width // head_count
    state_size = bc_stream.shape[1] // 2
    tap_count = conv_x.shape[0]
    blocks = row_count // SPAN
    edge_start = row_count - tap_count + 1
    own_ids = doc_ids.astype(jnp.float32)
    x_width = x_stream.shape[1]
    bc_width = bc_stream.shape[1]
    rim = from_behind(
        jnp.concatenate(
            [
                x_stream[edge_start:],
                bc_stream[edge_start:],
                jnp.broadcast_to(own_ids[edge_start:, None], (tap_count - 1, 128)).astype(
                    jnp.bfloat16
                ),
            ],
            axis=1,
        ),
        "seq",
        1,
    )
    rim_x = rim[:, :x_width]
    rim_bc = rim[:, x_width : x_width + bc_width]
    rim_ids = rim[:, x_width + bc_width]
    ext_ids = jnp.concatenate([rim_ids.astype(jnp.float32), own_ids])
    mixed_x = causal_conv(jnp.concatenate([rim_x, x_stream]), conv_x, ext_ids, own_ids, row_count)
    mixed_bc = causal_conv(
        jnp.concatenate([rim_bc, bc_stream]), conv_bc, ext_ids, own_ids, row_count
    )
    prior_id = ext_ids[tap_count - 2]
    step_size = jax.nn.softplus(dt_stream.astype(jnp.float32) + dt_bias[:, None])
    log_rates = -jnp.exp(a_log)[:, None] * step_size
    block_steps = step_size.reshape(head_count, blocks, SPAN)
    running = jnp.triu(jnp.ones((SPAN, SPAN), jnp.float32))
    cum_rates = jnp.einsum(
        "hcs,su->hcu",
        log_rates.reshape(head_count, blocks, SPAN),
        running,
        precision=lax.Precision.HIGHEST,
    )
    block_x = mixed_x.reshape(blocks, SPAN, head_count, head_size)
    b_vals = mixed_bc[:, :state_size].reshape(blocks, SPAN, state_size)
    c_vals = mixed_bc[:, state_size:].reshape(blocks, SPAN, state_size)
    c_wide = c_vals.astype(jnp.float32)
    block_ids = own_ids.reshape(blocks, SPAN)
    before = jnp.concatenate([prior_id[None], own_ids[SPAN - 1 :: SPAN][: blocks - 1]])
    carried = block_ids == before[:, None]
    entry_gain = jnp.where(carried[None], jnp.exp(cum_rates), 0.0)
    tail_weight = (
        jnp.where(
            (block_ids == block_ids[:, -1:])[None], jnp.exp(cum_rates[:, :, -1:] - cum_rates), 0.0
        )
        * block_steps
    )
    weighted = block_x.astype(jnp.float32) * jnp.transpose(tail_weight, (1, 2, 0))[..., None]
    block_states = jnp.einsum(
        "cshp,csn->chpn", weighted, b_vals.astype(jnp.float32), precision=highest
    )
    block_decay = jnp.where(carried[:, -1][None], jnp.exp(cum_rates[:, :, -1]), 0.0)
    device_decay = jnp.prod(block_decay, axis=1)
    skip_term = d_skip[None, None, :, None] * block_x.astype(jnp.float32)
    zero_state = jnp.zeros((head_count, head_size, state_size), jnp.float32)
    entry_list = [zero_state]
    for block in range(blocks):
        entry_list.append(block_decay[:, block, None, None] * entry_list[-1] + block_states[block])
    local_final = entry_list[-1]
    local_entries = jnp.stack(entry_list[:-1])
    reached = jnp.einsum("ctn,chpn->cthp", c_wide, local_entries, precision=highest)
    lower_mask = jnp.tril(jnp.ones((SPAN, SPAN), jnp.bool_))
    same_doc = (block_ids[:, :, None] == block_ids[:, None, :]) & lower_mask[None]
    spread = cum_rates[:, :, :, None] - cum_rates[:, :, None, :]
    decay_now = jnp.where(same_doc[None], jnp.exp(jnp.minimum(spread, 0.0)), 0.0)
    scores = jnp.einsum("ctn,csn->cts", c_vals, b_vals, preferred_element_type=jnp.float32)
    weights = (scores[None] * decay_now * block_steps[:, :, None, :]).astype(jnp.bfloat16)
    result = (
        jnp.einsum("hcts,cshp->cthp", weights, block_x, preferred_element_type=jnp.float32)
        + reached * jnp.transpose(entry_gain, (1, 2, 0))[..., None]
        + skip_term
    )
    incoming, (gate_silu, w_rows) = pass_state(
        device_decay,
        local_final,
        (z_gate, w_out),
        lambda pair: (jax.nn.silu(pair[0].astype(jnp.float32)), jnp.transpose(pair[1])),
    )
    prefix_list = [jnp.ones((head_count,), jnp.float32)]
    for block in range(blocks - 1):
        prefix_list.append(prefix_list[-1] * block_decay[:, block])
    prefix = jnp.stack(prefix_list, axis=1)
    reach_term = jnp.einsum("ctn,hpn->cthp", c_wide, incoming, precision=highest)
    result = (
        result + reach_term * jnp.transpose(entry_gain * prefix[:, :, None], (1, 2, 0))[..., None]
    )
    y_vals = result.reshape(row_count, inner_width).astype(jnp.bfloat16)
    gated = y_vals.astype(jnp.float32) * gate_silu
    group_count = lax.axis_size("tensor")
    squares = jnp.sum(gated * gated, axis=1)
    scaled = (gated * norm_gain[None, :]).astype(jnp.bfloat16)
    out_width = w_rows.shape[0] // group_count
    partial_value = jnp.einsum(
        "tc,gkc->gtk",
        scaled,
        w_rows.reshape(group_count, out_width, inner_width),
        preferred_element_type=jnp.float32,
    ).astype(jnp.bfloat16)
    square_column = jnp.broadcast_to(
        squares.astype(jnp.bfloat16)[None, :, None], (group_count, row_count, 1)
    )
    payload = jnp.concatenate([partial_value, square_column], axis=2)
    summed = lax.psum_scatter(payload, "tensor", scatter_dimension=0, tiled=True)[0]
    total_squares = summed[:, out_width].astype(jnp.float32)
    inv_norm = lax.rsqrt(total_squares / (inner_width * group_count) + 1e-05)
    return (summed[:, :out_width].astype(jnp.float32) * inv_norm[:, None]).astype(jnp.bfloat16)


def solution(mesh):
    return jax.shard_map(
        local,
        mesh=mesh,
        in_specs=(
            P(("dp", "seq"), "tensor"),
            P(("dp", "seq"), None),
            P(("dp", "seq"), "tensor"),
            P("tensor", ("dp", "seq")),
            P(("dp", "seq")),
            P(None, "tensor"),
            P(),
            P("tensor"),
            P("tensor"),
            P("tensor"),
            P("tensor"),
            P("tensor", None),
        ),
        out_specs=P(("dp", "seq"), "tensor"),
        check_vma=False,
    )
```

```python
import jax
import jax.numpy as jnp
from jax import lax
from jax.sharding import PartitionSpec as P

SPAN = 256


def from_behind(block, axis, distance):
    devices = range(lax.axis_size(axis))
    route = [(i - distance, i) for i in devices if i - distance in devices]
    return lax.ppermute(block, axis, route)


def causal_conv(extended, weights, ext_ids, own_ids, row_count):
    tap_count = weights.shape[0]
    total = jnp.zeros((row_count, extended.shape[1]), jnp.float32)
    for offset in range(tap_count):
        first_row = tap_count - 1 - offset
        window = extended[first_row : first_row + row_count]
        keep_mask = ext_ids[first_row : first_row + row_count] == own_ids
        total = total + jnp.where(
            keep_mask[:, None],
            window.astype(jnp.float32) * weights[offset].astype(jnp.float32),
            0.0,
        )
    return jax.nn.silu(total).astype(jnp.bfloat16)


def with_decay(decay, state):
    head_count = state.shape[0]
    high = decay.astype(jnp.bfloat16)
    low = (decay - high.astype(jnp.float32)).astype(jnp.bfloat16)
    tail_rows = -(-head_count // 16) * 16
    tail = jnp.pad(
        jnp.stack([high, low], 1), ((0, tail_rows - head_count), (0, state.shape[2] - 2))
    )
    flat = state.astype(jnp.bfloat16).reshape(head_count * state.shape[1], state.shape[2])
    return jnp.concatenate([flat, tail], axis=0)


def split_decay(packed, head_count, head_size):
    rows = head_count * head_size
    decay = packed[rows : rows + head_count, 0].astype(jnp.float32) + packed[
        rows : rows + head_count, 1
    ].astype(jnp.float32)
    return decay, packed[:rows].astype(jnp.float32).reshape(head_count, head_size, -1)


def pass_state(device_decay, local_final, passengers, prepare):
    shard_count = lax.axis_size("seq")
    decay, state = device_decay, local_final
    window = 1
    while 4 * window < shard_count - 1:
        sent = with_decay(decay, state)
        if window == 1:
            sent, passengers = lax.optimization_barrier((sent, passengers))
        received = from_behind(sent, "seq", window)
        if window == 1:
            received, passengers = lax.optimization_barrier((received, prepare(passengers)))
        prev_decay, prev_state = split_decay(received, *state.shape[:2])
        state = decay[:, None, None] * prev_state + state
        decay = decay * prev_decay
        window *= 2
    packed = with_decay(decay, state)
    part_count = -(-(shard_count - 1) // window)
    parts = [
        split_decay(from_behind(packed, "seq", 1 + part * window), *state.shape[:2])
        for part in range(part_count)
    ]
    if not parts:
        return jnp.zeros_like(local_final), passengers
    incoming_decay, incoming = parts[0]
    for part_decay, part_state in parts[1:]:
        incoming = incoming_decay[:, None, None] * part_state + incoming
        incoming_decay = incoming_decay * part_decay
    return incoming, passengers


def local(
    x_stream,
    bc_stream,
    z_gate,
    dt_stream,
    doc_ids,
    conv_x,
    conv_bc,
    a_log,
    dt_bias,
    d_skip,
    norm_gain,
    w_out,
):
    highest = lax.Precision.HIGHEST
    row_count = x_stream.shape[0]
    head_count = dt_stream.shape[0]
    inner_width = x_stream.shape[1]
    head_size = inner_width // head_count
    state_size = bc_stream.shape[1] // 2
    tap_count = conv_x.shape[0]
    blocks = row_count // SPAN
    edge_start = row_count - tap_count + 1
    own_ids = doc_ids.astype(jnp.float32)
    x_width = x_stream.shape[1]
    bc_width = bc_stream.shape[1]
    rim = from_behind(
        jnp.concatenate(
            [
                x_stream[edge_start:],
                bc_stream[edge_start:],
                jnp.broadcast_to(own_ids[edge_start:, None], (tap_count - 1, 128)).astype(
                    jnp.bfloat16
                ),
            ],
            axis=1,
        ),
        "seq",
        1,
    )
    rim_x = rim[:, :x_width]
    rim_bc = rim[:, x_width : x_width + bc_width]
    rim_ids = rim[:, x_width + bc_width]
    ext_ids = jnp.concatenate([rim_ids.astype(jnp.float32), own_ids])
    mixed_x = causal_conv(jnp.concatenate([rim_x, x_stream]), conv_x, ext_ids, own_ids, row_count)
    mixed_bc = causal_conv(
        jnp.concatenate([rim_bc, bc_stream]), conv_bc, ext_ids, own_ids, row_count
    )
    prior_id = ext_ids[tap_count - 2]
    step_size = jax.nn.softplus(dt_stream.astype(jnp.float32) + dt_bias[:, None])
    log_rates = -jnp.exp(a_log)[:, None] * step_size
    block_steps = step_size.reshape(head_count, blocks, SPAN)
    running = jnp.triu(jnp.ones((SPAN, SPAN), jnp.float32))
    cum_rates = jnp.einsum(
        "hcs,su->hcu",
        log_rates.reshape(head_count, blocks, SPAN),
        running,
        precision=lax.Precision.HIGHEST,
    )
    block_x = mixed_x.reshape(blocks, SPAN, head_count, head_size)
    b_vals = mixed_bc[:, :state_size].reshape(blocks, SPAN, state_size)
    c_vals = mixed_bc[:, state_size:].reshape(blocks, SPAN, state_size)
    c_wide = c_vals.astype(jnp.float32)
    block_ids = own_ids.reshape(blocks, SPAN)
    before = jnp.concatenate([prior_id[None], own_ids[SPAN - 1 :: SPAN][: blocks - 1]])
    carried = block_ids == before[:, None]
    entry_gain = jnp.where(carried[None], jnp.exp(cum_rates), 0.0)
    tail_weight = (
        jnp.where(
            (block_ids == block_ids[:, -1:])[None], jnp.exp(cum_rates[:, :, -1:] - cum_rates), 0.0
        )
        * block_steps
    )
    weighted = block_x.astype(jnp.float32) * jnp.transpose(tail_weight, (1, 2, 0))[..., None]
    block_states = jnp.einsum(
        "cshp,csn->chpn", weighted, b_vals.astype(jnp.float32), precision=highest
    )
    block_decay = jnp.where(carried[:, -1][None], jnp.exp(cum_rates[:, :, -1]), 0.0)
    device_decay = jnp.prod(block_decay, axis=1)
    skip_term = d_skip[None, None, :, None] * block_x.astype(jnp.float32)
    zero_state = jnp.zeros((head_count, head_size, state_size), jnp.float32)
    entry_list = [zero_state]
    for block in range(blocks):
        entry_list.append(block_decay[:, block, None, None] * entry_list[-1] + block_states[block])
    local_final = entry_list[-1]
    local_entries = jnp.stack(entry_list[:-1])
    reached = jnp.einsum("ctn,chpn->cthp", c_wide, local_entries, precision=highest)
    lower_mask = jnp.tril(jnp.ones((SPAN, SPAN), jnp.bool_))
    same_doc = (block_ids[:, :, None] == block_ids[:, None, :]) & lower_mask[None]
    spread = cum_rates[:, :, :, None] - cum_rates[:, :, None, :]
    decay_now = jnp.where(same_doc[None], jnp.exp(jnp.minimum(spread, 0.0)), 0.0)
    scores = jnp.einsum("ctn,csn->cts", c_vals, b_vals, preferred_element_type=jnp.float32)
    weights = (scores[None] * decay_now * block_steps[:, :, None, :]).astype(jnp.bfloat16)
    result = (
        jnp.einsum("hcts,cshp->cthp", weights, block_x, preferred_element_type=jnp.float32)
        + reached * jnp.transpose(entry_gain, (1, 2, 0))[..., None]
        + skip_term
    )
    incoming, (gate_silu, w_rows) = pass_state(
        device_decay,
        local_final,
        (z_gate, w_out),
        lambda pair: (jax.nn.silu(pair[0].astype(jnp.float32)), jnp.transpose(pair[1])),
    )
    prefix = jnp.cumprod(
        jnp.concatenate([jnp.ones((head_count, 1), jnp.float32), block_decay[:, :-1]], axis=1),
        axis=1,
    )
    incoming_high = incoming.astype(jnp.bfloat16)
    incoming_low = (incoming - incoming_high.astype(jnp.float32)).astype(jnp.bfloat16)
    reach_term = jnp.einsum(
        "ctn,hpn->cthp", c_vals, incoming_high, preferred_element_type=jnp.float32
    ) + jnp.einsum("ctn,hpn->cthp", c_vals, incoming_low, preferred_element_type=jnp.float32)
    result = (
        result + reach_term * jnp.transpose(entry_gain * prefix[:, :, None], (1, 2, 0))[..., None]
    )
    y_vals = result.reshape(row_count, inner_width).astype(jnp.bfloat16)
    gated = y_vals.astype(jnp.float32) * gate_silu
    group_count = lax.axis_size("tensor")
    squares = jnp.sum(gated * gated, axis=1)
    scaled = (gated * norm_gain[None, :]).astype(jnp.bfloat16)
    out_width = w_rows.shape[0] // group_count
    partial_value = jnp.einsum(
        "tc,gkc->gtk",
        scaled,
        w_rows.reshape(group_count, out_width, inner_width),
        preferred_element_type=jnp.float32,
    ).astype(jnp.bfloat16)
    square_column = jnp.broadcast_to(
        squares.astype(jnp.bfloat16)[None, :, None], (group_count, row_count, 1)
    )
    payload = jnp.concatenate([partial_value, square_column], axis=2)
    summed = lax.psum_scatter(payload, "tensor", scatter_dimension=0, tiled=True)[0]
    total_squares = summed[:, out_width].astype(jnp.float32)
    inv_norm = lax.rsqrt(total_squares / (inner_width * group_count) + 1e-05)
    return (summed[:, :out_width].astype(jnp.float32) * inv_norm[:, None]).astype(jnp.bfloat16)


def solution(mesh):
    return jax.shard_map(
        local,
        mesh=mesh,
        in_specs=(
            P(("dp", "seq"), "tensor"),
            P(("dp", "seq"), None),
            P(("dp", "seq"), "tensor"),
            P("tensor", ("dp", "seq")),
            P(("dp", "seq")),
            P(None, "tensor"),
            P(),
            P("tensor"),
            P("tensor"),
            P("tensor"),
            P("tensor"),
            P("tensor", None),
        ),
        out_specs=P(("dp", "seq"), "tensor"),
        check_vma=False,
    )
```
